256 devices in a mesh: lat: 32 (over z, x), lon: 8 (over y, core).
Axes of the slice: x: 4, y: 4, z: 8, core: 2. Of those that a mesh axis runs over, the one named last changes fastest.
Arguments:
- fields: bfloat16 [128, 720, 2, 512], P('lat', 'lon'), may hold values from -6 to 6
- coeffs: float32 [1024, 3], replicated, may hold values from -1.2 to 1.2
- entries: int32 [32, 4, 4, 128], replicated, may hold values from -3 to 1023, as said below
- band_info: int32 [32, 3], replicated, may hold values from 0 to 4, as said below
- conv_weight: bfloat16 [1536, 512], replicated, may hold values from -0.15625 to 0.15625
- mix_weight: bfloat16 [512, 512], replicated, may hold values from -0.25 to 0.25
Outputs:
- mixed: bfloat16 [128, 720, 2, 512], P('lat', 'lon')
The draws below stay inside these ranges and needn't reach their ends.
Inputs may be any that keep to these rules, and one draw needn't show every extreme that they name: `entries`: in band b's list every in row lies in b's own rows b * 4 to (b + 1) * 4 - 1, every out row differs from its in row by at most 3, shifts are 0 to 6 and filter rows 0 to 1023. `band_info`: count is 1 to 4 and equals 4 in the first and the last band; ext_lo and ext_hi are 0 to 3 and both equal 3 in bands 0, 1 and the last band.
All inputs are finite; a program needn't handle non-finite values.
Results may differ from the reference program's by a relative error of at most 0.0065.
Values may be sent and summed in bfloat16 or wider, within the bound.
No kernel may reach another device: no remote copies, remote signals or barrier semaphores. Data moves between devices by JAX's collectives and lax.ppermute only.
A program may use at most 128 MiB of HBM per device.

```python
import jax
import jax.numpy as jnp
from jax import lax

CHANNELS = 512
NLON = 720
MEMBERS = 2
BASIS = 3
SHIFTS = 7
OVERHANG = 3
BLOCKS = 4
FILTERS = 1024
LAT_DEV = 4
NBANDS = 32
NLAT = 128


def draw_entries(key, part):
    keys = jax.random.split(jax.random.fold_in(key, 11), 4)
    shape = (NBANDS, BLOCKS, 128)
    band_list = jnp.arange(NBANDS, dtype=jnp.int32)[:, None, None]
    in_rows = band_list * LAT_DEV + jax.random.randint(keys[0], shape, 0, LAT_DEV, dtype=jnp.int32)
    deltas = jax.random.randint(keys[1], shape, -OVERHANG, OVERHANG + 1, dtype=jnp.int32)
    out_rows = in_rows + deltas
    shifts = jax.random.randint(keys[2], shape, 0, SHIFTS, dtype=jnp.int32)
    filter_rows = jax.random.randint(keys[3], shape, 0, FILTERS, dtype=jnp.int32)
    return jnp.stack([out_rows, in_rows, shifts, filter_rows], axis=2).astype(jnp.int32)


def draw_band_info(key, part):
    keys = jax.random.split(jax.random.fold_in(key, 23), 2)
    band_list = jnp.arange(NBANDS, dtype=jnp.int32)
    distance = jnp.minimum(band_list, NBANDS - 1 - band_list)
    halfway = max(1, (NBANDS - 1) // 2)
    spare = jax.random.randint(keys[0], (NBANDS,), 0, BLOCKS, dtype=jnp.int32)
    counts = BLOCKS - spare * distance // halfway
    extents = jax.random.randint(keys[1], (NBANDS, 2), 0, OVERHANG + 1, dtype=jnp.int32)
    pinned = (band_list == 0) | (band_list == 1) | (band_list == NBANDS - 1)
    extents = jnp.where(pinned[:, None], OVERHANG, extents)
    return jnp.concatenate([counts[:, None], extents], axis=1).astype(jnp.int32)


def levels(own_key, dims, shards, smallest, high):
    level = 1.0
    for dim, parts in shards:
        steps = jax.random.uniform(jax.random.fold_in(jax.random.fold_in(own_key, 6), dim), (parts,), jnp.float32, smallest / len(shards), high / len(shards))
        level = level * jnp.repeat(jnp.exp(steps), dims[dim] // parts).reshape((-1,) + (1,) * (len(dims) - 1 - dim))
    return level


def bell_draw(own_key, shape, width, bound, cuts=(), kind=jnp.bfloat16):
    factor_of = levels(own_key, shape, cuts, -0.22, 0.18) if cuts else 1.0
    array = jax.random.normal(own_key, shape, jnp.float32) * width * factor_of
    return jnp.minimum(jnp.maximum(array, -bound), bound).astype(kind)


def setup_inputs(seed: int = 0) -> dict:
    splits = jax.random.split(jax.random.key(seed), 7)
    fields = bell_draw(splits[0], (NLAT, NLON, MEMBERS, CHANNELS), 1.0, 6.0, ((0, 32), (1, 8)))
    coeffs = bell_draw(splits[1], (FILTERS, BASIS), 0.2, 1.2, (), jnp.float32)
    entries = draw_entries(jax.random.fold_in(splits[6], 71), 0)
    band_info = draw_band_info(jax.random.fold_in(splits[6], 71), 0)
    conv_weight = bell_draw(splits[4], (BASIS * CHANNELS, CHANNELS), (BASIS * CHANNELS) ** -0.5, 0.15625)
    mix_weight = bell_draw(splits[5], (CHANNELS, CHANNELS), CHANNELS ** -0.5, 0.25)
    return {"fields": fields, "coeffs": coeffs, "entries": entries, "band_info": band_info, "conv_weight": conv_weight, "mix_weight": mix_weight}


def band_coupling(entries, band_meta, coeffs, band_index, out_start, out_count, in_start, in_count, band_rows, grid_rows):
    nbands = entries.shape[0]
    clamped = jnp.clip(band_index, 0, nbands - 1).astype(jnp.int32)
    listed = lax.dynamic_index_in_dim(entries, clamped, 0, keepdims=False)
    meta = lax.dynamic_index_in_dim(band_meta, clamped, 0, keepdims=False)
    blocks = listed.shape[0]
    flattened = jnp.transpose(listed, (1, 0, 2)).reshape(4, blocks * 128)
    out_rows = flattened[0]
    in_rows = flattened[1]
    shifts = flattened[2]
    filter_rows = flattened[3]
    block_ids = jnp.arange(blocks * 128, dtype=jnp.int32) // 128
    own_rel = out_rows - clamped * band_rows
    usable = (band_index >= 0) & (band_index < nbands) & (block_ids < meta[0])
    usable = usable & (own_rel >= -meta[1]) & (own_rel < band_rows + meta[2])
    usable = usable & (out_rows >= 0) & (out_rows < grid_rows)
    filter_pick = (filter_rows[:, None] == jnp.arange(coeffs.shape[0], dtype=jnp.int32)[None, :]).astype(jnp.float32)
    values = jnp.dot(filter_pick, coeffs, precision=lax.Precision.HIGHEST, preferred_element_type=jnp.float32)
    values = values * usable[:, None].astype(jnp.float32)
    out_hit = ((out_rows - out_start)[:, None] == jnp.arange(out_count, dtype=jnp.int32)[None, :]).astype(jnp.float32)
    basis = coeffs.shape[1]
    left_side = (out_hit[:, :, None] * values[:, None, :]).reshape(blocks * 128, out_count * basis)
    nshift = SHIFTS
    in_hit = ((shifts * in_count + in_rows - in_start)[:, None] == jnp.arange(nshift * in_count, dtype=jnp.int32)[None, :]).astype(jnp.float32)
    return jnp.dot(left_side.T, in_hit, precision=lax.Precision.HIGHEST, preferred_element_type=jnp.float32)


def reference(fields, coeffs, entries, band_info, conv_weight, mix_weight):
    kernel = conv_weight.reshape(BASIS, CHANNELS, CHANNELS).astype(jnp.float32)
    mixing = mix_weight.astype(jnp.float32)
    out_count = LAT_DEV + 2 * OVERHANG

    def band_rows_of(band_index):
        clamped = jnp.clip(band_index, 0, NBANDS - 1).astype(jnp.int32)
        band_fields = lax.dynamic_slice_in_dim(fields, (clamped * LAT_DEV).astype(jnp.int32), LAT_DEV, 0)
        coupling = band_coupling(entries, band_info, coeffs, band_index, band_index * LAT_DEV - OVERHANG, out_count,
                                 band_index * LAT_DEV, LAT_DEV, LAT_DEV, NLAT).astype(jnp.bfloat16)
        flattened = band_fields.reshape(LAT_DEV, NLON, MEMBERS * CHANNELS)
        stacked = jnp.concatenate([jnp.roll(flattened, offset, axis=1) for offset in range(SHIFTS)], axis=0)
        stacked = stacked.reshape(SHIFTS * LAT_DEV, NLON * MEMBERS * CHANNELS)
        result = jnp.dot(coupling, stacked, preferred_element_type=jnp.float32)
        return result.reshape(out_count, BASIS, NLON, MEMBERS, CHANNELS)

    def finish(middle):
        features = middle.astype(jnp.bfloat16).astype(jnp.float32)
        combined = jnp.einsum('lkomc,kcd->lomd', features, kernel)
        activated = jax.nn.gelu(combined, approximate=True).astype(jnp.bfloat16).astype(jnp.float32)
        return jnp.einsum('lomc,cd->lomd', activated, mixing).astype(jnp.bfloat16)

    def advance(carry, band_index):
        pending_mid, pending_up = carry
        extended = band_rows_of(band_index)
        finished = pending_mid + jnp.pad(extended[:OVERHANG], ((LAT_DEV - OVERHANG, 0), (0, 0), (0, 0), (0, 0), (0, 0)))
        emitted = finish(finished)
        new_mid = extended[OVERHANG:OVERHANG + LAT_DEV] + jnp.pad(pending_up, ((0, LAT_DEV - OVERHANG), (0, 0), (0, 0), (0, 0), (0, 0)))
        new_up = extended[OVERHANG + LAT_DEV:]
        return (new_mid, new_up), emitted

    start_mid = jnp.zeros((LAT_DEV, BASIS, NLON, MEMBERS, CHANNELS), jnp.float32)
    start_up = jnp.zeros((OVERHANG, BASIS, NLON, MEMBERS, CHANNELS), jnp.float32)
    band_list = jnp.arange(NBANDS + 1, dtype=jnp.int32)
    carry_out, emitted_all = lax.scan(advance, (start_mid, start_up), band_list)
    return emitted_all[1:].reshape(NLAT, NLON, MEMBERS, CHANNELS)
```

```python
import jax
import jax.numpy as jnp
from jax import lax
from jax.sharding import PartitionSpec as P

CHANNELS = 512
BASIS = 3
SHIFTS = 7
OVERHANG = 3
LAT_DEV = 4


def band_coupling(entries, band_meta, coeffs, band_index, grid_rows):
    nbands = entries.shape[0]
    blocks = entries.shape[1]
    ids = band_index + jnp.arange(-1, 2, dtype=jnp.int32)
    known = (ids >= 0) & (ids < nbands)
    clamped = jnp.clip(ids, 0, nbands - 1)
    listed = jnp.take(entries, clamped, axis=0)
    meta = jnp.take(band_meta, clamped, axis=0)
    out_rows = listed[:, :, 0, :]
    in_rows = listed[:, :, 1, :]
    shifts = listed[:, :, 2, :]
    filter_rows = listed[:, :, 3, :]
    block_ids = jnp.arange(blocks, dtype=jnp.int32)[None, :, None]
    own_rel = out_rows - clamped[:, None, None] * LAT_DEV
    usable = known[:, None, None] & (block_ids < meta[:, 0, None, None])
    usable = usable & (own_rel >= -meta[:, 1, None, None])
    usable = usable & (own_rel < LAT_DEV + meta[:, 2, None, None])
    usable = usable & (out_rows >= 0) & (out_rows < grid_rows)
    band_start = band_index * LAT_DEV
    q = (out_rows - band_start).reshape(-1)
    r = (in_rows - (band_start - OVERHANG)).reshape(-1)
    s = shifts.reshape(-1)
    values = jnp.take(coeffs, filter_rows.reshape(-1), axis=0)
    values = values * usable.reshape(-1)[:, None].astype(jnp.float32)
    out_hit = (q[:, None] == jnp.arange(LAT_DEV, dtype=jnp.int32)[None, :]).astype(jnp.float32)
    left_side = (out_hit[:, :, None] * values[:, None, :]).reshape(-1, LAT_DEV * BASIS)
    rows_in = LAT_DEV + 2 * OVERHANG
    in_hit = (
        (s * rows_in + r)[:, None] == jnp.arange(SHIFTS * rows_in, dtype=jnp.int32)[None, :]
    ).astype(jnp.float32)
    coupling = jnp.dot(
        left_side.T, in_hit, precision=lax.Precision.HIGHEST, preferred_element_type=jnp.float32
    )
    return coupling.reshape(LAT_DEV * BASIS, SHIFTS, rows_in)


def gather_rows(x):
    nlat = lax.axis_size("lat")
    nlon = lax.axis_size("lon")
    lo = SHIFTS - 1
    tail = x[:, x.shape[1] - lo :]

    def move(value, dlat, dlon):
        pairs = []
        for b in range(nlat):
            if 0 <= b + dlat < nlat:
                for j in range(nlon):
                    pairs.append((b * nlon + j, (b + dlat) * nlon + (j + dlon) % nlon))
        return lax.ppermute(value, ("lat", "lon"), pairs)

    below = move(x[LAT_DEV - OVERHANG :], 1, 0)
    above = move(x[:OVERHANG], -1, 0)
    left = move(tail, 0, 1)
    below_left = move(tail[LAT_DEV - OVERHANG :], 1, 1)
    above_left = move(tail[:OVERHANG], -1, 1)
    rows_below = jnp.concatenate([below_left, below], axis=1)
    rows_mid = jnp.concatenate([left, x], axis=1)
    rows_above = jnp.concatenate([above_left, above], axis=1)
    return jnp.concatenate([rows_below, rows_mid, rows_above], axis=0)


def shards(fields, coeffs, entries, band_info, conv_weight, mix_weight):
    band_index = lax.axis_index("lat")
    grid_rows = LAT_DEV * lax.axis_size("lat")
    nrows, nlon, members, channels = fields.shape
    coupling = band_coupling(entries, band_info, coeffs, band_index, grid_rows).astype(jnp.bfloat16)
    rows = gather_rows(fields)
    ext = rows.shape[1]
    lo = SHIFTS - 1
    pick = (
        jnp.arange(ext, dtype=jnp.int32)[None, None, :]
        == jnp.arange(nlon, dtype=jnp.int32)[None, :, None]
        + lo
        - jnp.arange(SHIFTS, dtype=jnp.int32)[:, None, None]
    ).astype(jnp.bfloat16)
    toeplitz = jnp.einsum(
        "asr,slt->alrt", coupling, pick, preferred_element_type=jnp.float32
    ).astype(jnp.bfloat16)
    rows_in = rows.shape[0]
    toeplitz = toeplitz.reshape(LAT_DEV * BASIS * nlon, rows_in * ext)
    conv = jnp.dot(
        toeplitz, rows.reshape(rows_in * ext, members * channels), preferred_element_type=jnp.float32
    )
    features = conv.astype(jnp.bfloat16).reshape(LAT_DEV, BASIS, nlon, members, channels)
    kernel = conv_weight.reshape(BASIS, CHANNELS, CHANNELS)
    combined = jnp.einsum("qklmc,kcd->qlmd", features, kernel, preferred_element_type=jnp.float32)
    activated = jax.nn.gelu(combined, approximate=True).astype(jnp.bfloat16)
    return jnp.einsum(
        "qlmc,cd->qlmd", activated, mix_weight, preferred_element_type=jnp.float32
    ).astype(jnp.bfloat16)


def solution(mesh):
    in_specs = (P("lat", "lon", None, None), P(), P(), P(), P(), P())
    out_specs = P("lat", "lon", None, None)
    return jax.shard_map(shards, mesh=mesh, in_specs=in_specs, out_specs=out_specs, check_vma=False)
```

```python
import jax
import jax.numpy as jnp
from jax import lax
from jax.experimental import pallas as pl
from jax.experimental.pallas import tpu as pltpu
from jax.sharding import PartitionSpec as P

CHANNELS = 512
BASIS = 3
SHIFTS = 7
OVERHANG = 3
LAT_DEV = 4


def band_coupling(entries, band_meta, coeffs, band_index, grid_rows):
    nbands = entries.shape[0]
    blocks = entries.shape[1]
    ids = band_index + jnp.arange(-1, 2, dtype=jnp.int32)
    known = (ids >= 0) & (ids < nbands)
    clamped = jnp.clip(ids, 0, nbands - 1)
    listed = jnp.take(entries, clamped, axis=0)
    meta = jnp.take(band_meta, clamped, axis=0)
    out_rows = listed[:, :, 0, :]
    in_rows = listed[:, :, 1, :]
    shifts = listed[:, :, 2, :]
    filter_rows = listed[:, :, 3, :]
    block_ids = jnp.arange(blocks, dtype=jnp.int32)[None, :, None]
    own_rel = out_rows - clamped[:, None, None] * LAT_DEV
    usable = known[:, None, None] & (block_ids < meta[:, 0, None, None])
    usable = usable & (own_rel >= -meta[:, 1, None, None])
    usable = usable & (own_rel < LAT_DEV + meta[:, 2, None, None])
    usable = usable & (out_rows >= 0) & (out_rows < grid_rows)
    band_start = band_index * LAT_DEV
    rows_in = LAT_DEV + 2 * OVERHANG
    q = out_rows - band_start
    r = in_rows - (band_start - OVERHANG)
    usable = usable & (q >= 0) & (q < LAT_DEV) & (r >= 0) & (r < rows_in)
    slot = jnp.where(usable, (q * SHIFTS + shifts) * rows_in + r, -1).reshape(-1)
    nslots = LAT_DEV * SHIFTS * rows_in
    slot_hit = (slot[:, None] == jnp.arange(nslots, dtype=jnp.int32)[None, :]).astype(jnp.bfloat16)
    nfilters = coeffs.shape[0]
    filter_hit = (
        filter_rows.reshape(-1)[:, None] == jnp.arange(nfilters, dtype=jnp.int32)[None, :]
    ).astype(jnp.bfloat16)
    counts = lax.dot_general(
        filter_hit, slot_hit, (((0,), (0,)), ((), ())), preferred_element_type=jnp.float32
    )
    coupling = jnp.dot(
        coeffs.T, counts, precision=lax.Precision.HIGHEST, preferred_element_type=jnp.float32
    )
    return coupling.reshape(BASIS, LAT_DEV, SHIFTS, rows_in)


def gather_rows(x):
    nlat = lax.axis_size("lat")
    nlon = lax.axis_size("lon")
    lo = SHIFTS - 1
    tail = x[:, x.shape[1] - lo :]

    def move(value, dlat, dlon):
        pairs = []
        for b in range(nlat):
            if 0 <= b + dlat < nlat:
                for j in range(nlon):
                    pairs.append((b * nlon + j, (b + dlat) * nlon + (j + dlon) % nlon))
        return lax.ppermute(value, ("lat", "lon"), pairs)

    below = move(x[LAT_DEV - OVERHANG :], 1, 0)
    above = move(x[:OVERHANG], -1, 0)
    left = move(tail, 0, 1)
    below_left = move(tail[LAT_DEV - OVERHANG :], 1, 1)
    above_left = move(tail[:OVERHANG], -1, 1)
    rows_below = jnp.concatenate([below_left, below], axis=1)
    rows_mid = jnp.concatenate([left, x], axis=1)
    rows_above = jnp.concatenate([above_left, above], axis=1)
    return jnp.concatenate([rows_below, rows_mid, rows_above], axis=0)


WINDOW = 30
ROW_PAD = 16


def conv_mix_kernel(toeplitz_ref, rows_ref, weight_ref, mix_ref, out_ref):
    nwin = out_ref.shape[0] // (2 * WINDOW * LAT_DEV)
    span = WINDOW * LAT_DEV
    pieces = [[[] for _ in range(2)] for _ in range(BASIS)]
    for j in range(nwin):
        window = rows_ref[pl.ds(j * WINDOW * ROW_PAD, (WINDOW + SHIFTS - 1) * ROW_PAD), :]
        conv = jnp.dot(toeplitz_ref[...], window, preferred_element_type=jnp.float32)
        for k in range(BASIS):
            for m in range(2):
                pieces[k][m].append(conv[k * span : (k + 1) * span, m * CHANNELS : (m + 1) * CHANNELS])
    combined = None
    for k in range(BASIS):
        features = jnp.concatenate(pieces[k][0] + pieces[k][1], axis=0).astype(jnp.bfloat16)
        term = jnp.dot(
            features,
            weight_ref[k * CHANNELS : (k + 1) * CHANNELS, :],
            preferred_element_type=jnp.float32,
        )
        combined = term if combined is None else combined + term
    activated = jax.nn.gelu(combined, approximate=True).astype(jnp.bfloat16)
    out_ref[...] = jnp.dot(activated, mix_ref[...], preferred_element_type=jnp.float32).astype(
        out_ref.dtype
    )


def shards(fields, coeffs, entries, band_info, conv_weight, mix_weight):
    band_index = lax.axis_index("lat")
    grid_rows = LAT_DEV * lax.axis_size("lat")
    nrows, nlon, members, channels = fields.shape
    lo = SHIFTS - 1
    coupling = band_coupling(entries, band_info, coeffs, band_index, grid_rows).astype(jnp.bfloat16)
    rows = gather_rows(fields)
    rows_in, ext = rows.shape[0], rows.shape[1]
    rows = jnp.pad(rows, ((0, ROW_PAD - rows_in), (0, 0), (0, 0), (0, 0)))
    rows = jnp.transpose(rows, (1, 0, 2, 3)).reshape(ext * ROW_PAD, members * channels)
    pick = (
        jnp.arange(WINDOW + lo, dtype=jnp.int32)[None, None, :]
        == jnp.arange(WINDOW, dtype=jnp.int32)[None, :, None]
        + lo
        - jnp.arange(SHIFTS, dtype=jnp.int32)[:, None, None]
    ).astype(jnp.bfloat16)
    toeplitz = jnp.einsum("kqsr,slt->klqtr", coupling, pick, preferred_element_type=jnp.float32)
    toeplitz = jnp.pad(toeplitz, ((0, 0),) * 4 + ((0, ROW_PAD - rows_in),)).astype(jnp.bfloat16)
    toeplitz = toeplitz.reshape(BASIS * WINDOW * LAT_DEV, (WINDOW + lo) * ROW_PAD)
    out_rows = members * nlon * LAT_DEV
    mixed = pl.pallas_call(
        conv_mix_kernel,
        out_shape=jax.ShapeDtypeStruct((out_rows, CHANNELS), jnp.bfloat16),
        in_specs=[pl.BlockSpec(memory_space=pltpu.VMEM)] * 4,
        out_specs=pl.BlockSpec(memory_space=pltpu.VMEM),
        cost_estimate=pl.CostEstimate(
            flops=2 * toeplitz.shape[0] * toeplitz.shape[1] * 1024 * (nlon // WINDOW)
            + 2 * out_rows * CHANNELS * CHANNELS * (BASIS + 1),
            transcendentals=out_rows * CHANNELS,
            bytes_accessed=rows.size * 2 + toeplitz.size * 2 + (BASIS + 2) * CHANNELS * CHANNELS * 2,
        ),
    )(toeplitz, rows, conv_weight, mix_weight)
    return jnp.transpose(mixed.reshape(members, nlon, LAT_DEV, CHANNELS), (2, 1, 0, 3))


def solution(mesh):
    in_specs = (P("lat", "lon", None, None), P(), P(), P(), P(), P())
    out_specs = P("lat", "lon", None, None)
    return jax.shard_map(shards, mesh=mesh, in_specs=in_specs, out_specs=out_specs, check_vma=False)
```

```python
import jax
import jax.numpy as jnp
from jax import lax
from jax.experimental import pallas as pl
from jax.experimental.pallas import tpu as pltpu
from jax.sharding import PartitionSpec as P

CHANNELS = 512
BASIS = 3
SHIFTS = 7
OVERHANG = 3
LAT_DEV = 4
ROW_PAD = 16


def band_coupling(entries, band_meta, coeffs, band_index, grid_rows):
    nbands = entries.shape[0]
    blocks = entries.shape[1]
    ids = band_index + jnp.arange(-1, 2, dtype=jnp.int32)
    known = (ids >= 0) & (ids < nbands)
    clamped = jnp.clip(ids, 0, nbands - 1)
    listed = jnp.take(entries, clamped, axis=0)
    meta = jnp.take(band_meta, clamped, axis=0)
    out_rows = listed[:, :, 0, :]
    in_rows = listed[:, :, 1, :]
    shifts = listed[:, :, 2, :]
    filter_rows = listed[:, :, 3, :]
    block_ids = jnp.arange(blocks, dtype=jnp.int32)[None, :, None]
    own_rel = out_rows - clamped[:, None, None] * LAT_DEV
    usable = known[:, None, None] & (block_ids < meta[:, 0, None, None])
    usable = usable & (own_rel >= -meta[:, 1, None, None])
    usable = usable & (own_rel < LAT_DEV + meta[:, 2, None, None])
    usable = usable & (out_rows >= 0) & (out_rows < grid_rows)
    band_start = band_index * LAT_DEV
    rows_in = LAT_DEV + 2 * OVERHANG
    q = out_rows - band_start
    r = in_rows - (band_start - OVERHANG)
    usable = usable & (q >= 0) & (q < LAT_DEV) & (r >= 0) & (r < rows_in)
    slot = jnp.where(usable, q * 128 + (SHIFTS - 1 - shifts) * ROW_PAD + r, -1).reshape(-1)
    nslots = LAT_DEV * 128
    slot_hit = (slot[:, None] == jnp.arange(nslots, dtype=jnp.int32)[None, :]).astype(jnp.bfloat16)
    nfilters = coeffs.shape[0]
    filter_hit = (
        filter_rows.reshape(-1)[:, None] == jnp.arange(nfilters, dtype=jnp.int32)[None, :]
    ).astype(jnp.bfloat16)
    counts = lax.dot_general(
        filter_hit, slot_hit, (((0,), (0,)), ((), ())), preferred_element_type=jnp.float32
    )
    coupling = jnp.dot(
        coeffs.T, counts, precision=lax.Precision.HIGHEST, preferred_element_type=jnp.float32
    )
    return coupling


def gather_rows(x):
    nlat = lax.axis_size("lat")
    nlon = lax.axis_size("lon")
    lo = SHIFTS - 1
    tail = x[:, x.shape[1] - lo :]

    def move(value, dlat, dlon):
        pairs = []
        for b in range(nlat):
            if 0 <= b + dlat < nlat:
                for j in range(nlon):
                    pairs.append((b * nlon + j, (b + dlat) * nlon + (j + dlon) % nlon))
        return lax.ppermute(value, ("lat", "lon"), pairs)

    below = move(x[LAT_DEV - OVERHANG :], 1, 0)
    above = move(x[:OVERHANG], -1, 0)
    left = move(tail, 0, 1)
    below_left = move(tail[LAT_DEV - OVERHANG :], 1, 1)
    above_left = move(tail[:OVERHANG], -1, 1)
    rows_below = jnp.concatenate([below_left, below], axis=1)
    rows_mid = jnp.concatenate([left, x], axis=1)
    rows_above = jnp.concatenate([above_left, above], axis=1)
    return jnp.concatenate([rows_below, rows_mid, rows_above], axis=0)


WINDOW = 30
LON_PAD = 32
TAPS = 128


def conv_mix_kernel(coupling_ref, rows_ref, weight_ref, mix_ref, out_ref, toeplitz_ref):
    lo = SHIFTS - 1
    cols = (WINDOW + lo + 4) * ROW_PAD
    for k in range(BASIS):
        for q in range(LAT_DEV):
            taps = coupling_ref[k : k + 1, q * TAPS : (q + 1) * TAPS]
            wide = jnp.concatenate([taps, jnp.zeros((1, cols - TAPS), jnp.float32)], axis=1)
            block = jnp.broadcast_to(wide, (LON_PAD, cols))
            block = pltpu.roll(block, 0, 1, stride=ROW_PAD, stride_axis=0)
            toeplitz_ref[pl.ds((k * LAT_DEV + q) * LON_PAD, LON_PAD), :] = block.astype(jnp.bfloat16)
    nwin = out_ref.shape[0] // (2 * LAT_DEV * LON_PAD)
    span = LAT_DEV * LON_PAD
    pieces = [[[] for _ in range(2)] for _ in range(BASIS)]
    for j in range(nwin):
        window = rows_ref[pl.ds(j * WINDOW, cols // ROW_PAD), :, :].reshape(cols, 2 * CHANNELS)
        conv = jnp.dot(toeplitz_ref[...], window, preferred_element_type=jnp.float32)
        for k in range(BASIS):
            for m in range(2):
                pieces[k][m].append(conv[k * span : (k + 1) * span, m * CHANNELS : (m + 1) * CHANNELS])
    combined = None
    for k in range(BASIS):
        features = jnp.concatenate(pieces[k][0] + pieces[k][1], axis=0).astype(jnp.bfloat16)
        term = jnp.dot(
            features,
            weight_ref[k * CHANNELS : (k + 1) * CHANNELS, :],
            preferred_element_type=jnp.float32,
        )
        combined = term if combined is None else combined + term
    activated = jax.nn.gelu(combined, approximate=True).astype(jnp.bfloat16)
    out_ref[...] = jnp.dot(activated, mix_ref[...], preferred_element_type=jnp.float32).astype(
        out_ref.dtype
    )


def shards(fields, coeffs, entries, band_info, conv_weight, mix_weight):
    band_index = lax.axis_index("lat")
    grid_rows = LAT_DEV * lax.axis_size("lat")
    nrows, nlon, members, channels = fields.shape
    lo = SHIFTS - 1
    coupling = band_coupling(entries, band_info, coeffs, band_index, grid_rows)
    coupling = coupling.astype(jnp.bfloat16).astype(jnp.float32)
    rows = gather_rows(fields)
    rows_in, ext = rows.shape[0], rows.shape[1]
    nwin = nlon // WINDOW
    cols = (WINDOW + lo + 4) * ROW_PAD
    lon_rows = (nwin - 1) * WINDOW + cols // ROW_PAD
    rows = jnp.pad(rows, ((0, ROW_PAD - rows_in), (0, lon_rows - ext), (0, 0), (0, 0)))
    rows = jnp.transpose(rows, (1, 0, 2, 3)).reshape(lon_rows, ROW_PAD, members * channels)
    out_rows = members * nwin * LAT_DEV * LON_PAD
    mixed = pl.pallas_call(
        conv_mix_kernel,
        out_shape=jax.ShapeDtypeStruct((out_rows, CHANNELS), jnp.bfloat16),
        in_specs=[pl.BlockSpec(memory_space=pltpu.VMEM)] * 4,
        out_specs=pl.BlockSpec(memory_space=pltpu.VMEM),
        scratch_shapes=[pltpu.VMEM((BASIS * LAT_DEV * LON_PAD, cols), jnp.bfloat16)],
        cost_estimate=pl.CostEstimate(
            flops=2 * BASIS * LAT_DEV * LON_PAD * cols * 1024 * nwin
            + 2 * out_rows * CHANNELS * CHANNELS * (BASIS + 1),
            transcendentals=out_rows * CHANNELS,
            bytes_accessed=rows.size * 2 + (BASIS + 2) * CHANNELS * CHANNELS * 2,
        ),
    )(coupling, rows, conv_weight, mix_weight)
    mixed = mixed.reshape(members, nwin, LAT_DEV, LON_PAD, CHANNELS)[:, :, :, :WINDOW]
    return jnp.transpose(mixed, (2, 1, 3, 0, 4)).reshape(LAT_DEV, nlon, members, CHANNELS)


def solution(mesh):
    in_specs = (P("lat", "lon", None, None), P(), P(), P(), P(), P())
    out_specs = P("lat", "lon", None, None)
    return jax.shard_map(shards, mesh=mesh, in_specs=in_specs, out_specs=out_specs, check_vma=False)
```

```python
import jax
import jax.numpy as jnp
from jax import lax
from jax.experimental import pallas as pl
from jax.experimental.pallas import tpu as pltpu
from jax.sharding import PartitionSpec as P

CHANNELS = 512
BASIS = 3
SHIFTS = 7
OVERHANG = 3
LAT_DEV = 4
ROW_PAD = 10


def band_coupling(entries, band_meta, coeffs, band_index, grid_rows):
    nbands = entries.shape[0]
    blocks = entries.shape[1]
    ids = band_index + jnp.arange(-1, 2, dtype=jnp.int32)
    known = (ids >= 0) & (ids < nbands)
    clamped = jnp.clip(ids, 0, nbands - 1)
    listed = jnp.take(entries, clamped, axis=0)
    meta = jnp.take(band_meta, clamped, axis=0)
    out_rows = listed[:, :, 0, :]
    in_rows = listed[:, :, 1, :]
    shifts = listed[:, :, 2, :]
    filter_rows = listed[:, :, 3, :]
    block_ids = jnp.arange(blocks, dtype=jnp.int32)[None, :, None]
    own_rel = out_rows - clamped[:, None, None] * LAT_DEV
    usable = known[:, None, None] & (block_ids < meta[:, 0, None, None])
    usable = usable & (own_rel >= -meta[:, 1, None, None])
    usable = usable & (own_rel < LAT_DEV + meta[:, 2, None, None])
    usable = usable & (out_rows >= 0) & (out_rows < grid_rows)
    band_start = band_index * LAT_DEV
    rows_in = LAT_DEV + 2 * OVERHANG
    q = out_rows - band_start
    r = in_rows - (band_start - OVERHANG)
    usable = usable & (q >= 0) & (q < LAT_DEV) & (r >= 0) & (r < rows_in)
    slot = jnp.where(usable, q * 128 + (SHIFTS - 1 - shifts) * ROW_PAD + r, -1).reshape(-1)
    nslots = LAT_DEV * 128
    slot_hit = (slot[:, None] == jnp.arange(nslots, dtype=jnp.int32)[None, :]).astype(jnp.bfloat16)
    nfilters = coeffs.shape[0]
    filter_hit = (
        filter_rows.reshape(-1)[:, None] == jnp.arange(nfilters, dtype=jnp.int32)[None, :]
    ).astype(jnp.bfloat16)
    counts = lax.dot_general(
        filter_hit, slot_hit, (((0,), (0,)), ((), ())), preferred_element_type=jnp.float32
    )
    coupling = jnp.dot(
        coeffs.T, counts, precision=lax.Precision.HIGHEST, preferred_element_type=jnp.float32
    )
    return coupling


def gather_rows(x):
    nlat = lax.axis_size("lat")
    nlon = lax.axis_size("lon")
    lo = SHIFTS - 1
    tail = x[:, x.shape[1] - lo :]

    def move(value, dlat, dlon):
        pairs = []
        for b in range(nlat):
            if 0 <= b + dlat < nlat:
                for j in range(nlon):
                    pairs.append((b * nlon + j, (b + dlat) * nlon + (j + dlon) % nlon))
        return lax.ppermute(value, ("lat", "lon"), pairs)

    below = move(x[LAT_DEV - OVERHANG :], 1, 0)
    above = move(x[:OVERHANG], -1, 0)
    left = move(tail, 0, 1)
    below_left = move(tail[LAT_DEV - OVERHANG :], 1, 1)
    above_left = move(tail[:OVERHANG], -1, 1)
    rows_below = jnp.concatenate([below_left, below], axis=1)
    rows_mid = jnp.concatenate([left, x], axis=1)
    rows_above = jnp.concatenate([above_left, above], axis=1)
    return jnp.concatenate([rows_below, rows_mid, rows_above], axis=0)


WINDOW = 32
LON_PAD = 32
TAPS = 128
DEPTH = 384


def conv_mix_kernel(coupling_ref, rows_ref, weight_ref, mix_ref, out_ref, toeplitz_ref):
    for k in range(BASIS):
        for q in range(LAT_DEV):
            taps = coupling_ref[k : k + 1, q * TAPS : (q + 1) * TAPS]
            wide = jnp.concatenate([taps, jnp.zeros((1, DEPTH - TAPS), jnp.float32)], axis=1)
            for g in range(LON_PAD // 8):
                block = jnp.broadcast_to(wide, (8, DEPTH))
                if g:
                    block = pltpu.roll(block, 8 * g * ROW_PAD, 1)
                block = pltpu.roll(block, 0, 1, stride=ROW_PAD, stride_axis=0)
                toeplitz_ref[pl.ds((k * LAT_DEV + q) * LON_PAD + 8 * g, 8), :] = block.astype(
                    jnp.bfloat16
                )
    nwin = out_ref.shape[0] // (2 * LAT_DEV * LON_PAD)
    span = LAT_DEV * LON_PAD
    pieces = [[[] for _ in range(2)] for _ in range(BASIS)]
    for j in range(nwin):
        window = rows_ref[pl.ds(j * WINDOW * ROW_PAD, DEPTH), :]
        conv = jnp.dot(toeplitz_ref[...], window, preferred_element_type=jnp.float32)
        for k in range(BASIS):
            for m in range(2):
                pieces[k][m].append(conv[k * span : (k + 1) * span, m * CHANNELS : (m + 1) * CHANNELS])
    combined = None
    for k in range(BASIS):
        features = jnp.concatenate(pieces[k][0] + pieces[k][1], axis=0).astype(jnp.bfloat16)
        term = jnp.dot(
            features,
            weight_ref[k * CHANNELS : (k + 1) * CHANNELS, :],
            preferred_element_type=jnp.float32,
        )
        combined = term if combined is None else combined + term
    activated = jax.nn.gelu(combined, approximate=True).astype(jnp.bfloat16)
    out_ref[...] = jnp.dot(activated, mix_ref[...], preferred_element_type=jnp.float32).astype(
        out_ref.dtype
    )


def shards(fields, coeffs, entries, band_info, conv_weight, mix_weight):
    band_index = lax.axis_index("lat")
    grid_rows = LAT_DEV * lax.axis_size("lat")
    nrows, nlon, members, channels = fields.shape
    coupling = band_coupling(entries, band_info, coeffs, band_index, grid_rows)
    coupling = coupling.astype(jnp.bfloat16).astype(jnp.float32)
    rows = gather_rows(fields)
    rows_in, ext = rows.shape[0], rows.shape[1]
    nwin = -(-nlon // WINDOW)
    depth_rows = (nwin - 1) * WINDOW * ROW_PAD + DEPTH
    rows = jnp.transpose(rows, (1, 0, 2, 3)).reshape(ext * rows_in, members * channels)
    rows = jnp.pad(rows, ((0, depth_rows - ext * rows_in), (0, 0)))
    out_rows = members * nwin * LAT_DEV * LON_PAD
    mixed = pl.pallas_call(
        conv_mix_kernel,
        out_shape=jax.ShapeDtypeStruct((out_rows, CHANNELS), jnp.bfloat16),
        in_specs=[pl.BlockSpec(memory_space=pltpu.VMEM)] * 4,
        out_specs=pl.BlockSpec(memory_space=pltpu.VMEM),
        scratch_shapes=[pltpu.VMEM((BASIS * LAT_DEV * LON_PAD, DEPTH), jnp.bfloat16)],
        cost_estimate=pl.CostEstimate(
            flops=2 * BASIS * LAT_DEV * LON_PAD * DEPTH * 1024 * nwin
            + 2 * out_rows * CHANNELS * CHANNELS * (BASIS + 1),
            transcendentals=out_rows * CHANNELS,
            bytes_accessed=rows.size * 2 + (BASIS + 2) * CHANNELS * CHANNELS * 2,
        ),
    )(coupling, rows, conv_weight, mix_weight)
    mixed = mixed.reshape(members, nwin, LAT_DEV, LON_PAD, CHANNELS)
    mixed = jnp.transpose(mixed, (2, 1, 3, 0, 4)).reshape(LAT_DEV, nwin * LON_PAD, members, CHANNELS)
    return mixed[:, :nlon]


def solution(mesh):
    in_specs = (P("lat", "lon", None, None), P(), P(), P(), P(), P())
    out_specs = P("lat", "lon", None, None)
    return jax.shard_map(shards, mesh=mesh, in_specs=in_specs, out_specs=out_specs, check_vma=False)
```

```python
import jax
import jax.numpy as jnp
from jax import lax
from jax.experimental import pallas as pl
from jax.experimental.pallas import tpu as pltpu
from jax.sharding import PartitionSpec as P

CHANNELS = 512
BASIS = 3
SHIFTS = 7
OVERHANG = 3
LAT_DEV = 4
ROW_PAD = 10


def band_coupling(entries, band_meta, coeffs, band_index, grid_rows):
    nbands = entries.shape[0]
    blocks = entries.shape[1]
    ids = band_index + jnp.arange(-1, 2, dtype=jnp.int32)
    known = (ids >= 0) & (ids < nbands)
    clamped = jnp.clip(ids, 0, nbands - 1)
    listed = jnp.take(entries, clamped, axis=0)
    meta = jnp.take(band_meta, clamped, axis=0)
    out_rows = listed[:, :, 0, :]
    in_rows = listed[:, :, 1, :]
    shifts = listed[:, :, 2, :]
    filter_rows = listed[:, :, 3, :]
    block_ids = jnp.arange(blocks, dtype=jnp.int32)[None, :, None]
    own_rel = out_rows - clamped[:, None, None] * LAT_DEV
    usable = known[:, None, None] & (block_ids < meta[:, 0, None, None])
    usable = usable & (own_rel >= -meta[:, 1, None, None])
    usable = usable & (own_rel < LAT_DEV + meta[:, 2, None, None])
    usable = usable & (out_rows >= 0) & (out_rows < grid_rows)
    band_start = band_index * LAT_DEV
    rows_in = LAT_DEV + 2 * OVERHANG
    q = out_rows - band_start
    r = in_rows - (band_start - OVERHANG)
    usable = usable & (q >= 0) & (q < LAT_DEV) & (r >= 0) & (r < rows_in)
    slot = jnp.where(usable, q * 128 + (SHIFTS - 1 - shifts) * ROW_PAD + r, -1).reshape(-1)
    nslots = LAT_DEV * 128
    slot_hit = (slot[:, None] == jnp.arange(nslots, dtype=jnp.int32)[None, :]).astype(jnp.bfloat16)
    nfilters = coeffs.shape[0]
    filter_hit = (
        filter_rows.reshape(-1)[:, None] == jnp.arange(nfilters, dtype=jnp.int32)[None, :]
    ).astype(jnp.bfloat16)
    counts = lax.dot_general(
        filter_hit, slot_hit, (((0,), (0,)), ((), ())), preferred_element_type=jnp.float32
    )
    coupling = jnp.dot(
        coeffs.T, counts, precision=lax.Precision.HIGHEST, preferred_element_type=jnp.float32
    )
    return coupling


def gather_rows(x):
    nlat = lax.axis_size("lat")
    nlon = lax.axis_size("lon")
    lo = SHIFTS - 1
    down = [(b, b + 1) for b in range(nlat - 1)]
    below = lax.ppermute(x[LAT_DEV - OVERHANG :], "lat", down)
    above = lax.ppermute(x[:OVERHANG], "lat", [(t, s) for s, t in down])
    rows = jnp.concatenate([below, x, above], axis=0)
    tail = lax.ppermute(rows[:, x.shape[1] - lo :], "lon", [(j, (j + 1) % nlon) for j in range(nlon)])
    return jnp.concatenate([tail, rows], axis=1)


WINDOW = 32
LON_PAD = 32
TAPS = 128
DEPTH = 384


def conv_mix_kernel(coupling_ref, rows_ref, weight_ref, mix_ref, out_ref, toeplitz_ref):
    for k in range(BASIS):
        for q in range(LAT_DEV):
            taps = coupling_ref[k : k + 1, q * TAPS : (q + 1) * TAPS]
            wide = jnp.concatenate([taps, jnp.zeros((1, DEPTH - TAPS), jnp.float32)], axis=1)
            for g in range(LON_PAD // 8):
                block = jnp.broadcast_to(wide, (8, DEPTH))
                if g:
                    block = pltpu.roll(block, 8 * g * ROW_PAD, 1)
                block = pltpu.roll(block, 0, 1, stride=ROW_PAD, stride_axis=0)
                toeplitz_ref[pl.ds((k * LAT_DEV + q) * LON_PAD + 8 * g, 8), :] = block.astype(
                    jnp.bfloat16
                )
    nwin = out_ref.shape[0] // (2 * LAT_DEV * LON_PAD)
    span = LAT_DEV * LON_PAD
    pieces = [[[] for _ in range(2)] for _ in range(BASIS)]
    for j in range(nwin):
        window = rows_ref[pl.ds(j * WINDOW * ROW_PAD, DEPTH), :]
        conv = jnp.dot(toeplitz_ref[...], window, preferred_element_type=jnp.float32)
        for k in range(BASIS):
            for m in range(2):
                pieces[k][m].append(conv[k * span : (k + 1) * span, m * CHANNELS : (m + 1) * CHANNELS])
    combined = None
    for k in range(BASIS):
        features = jnp.concatenate(pieces[k][0] + pieces[k][1], axis=0).astype(jnp.bfloat16)
        term = jnp.dot(
            features,
            weight_ref[k * CHANNELS : (k + 1) * CHANNELS, :],
            preferred_element_type=jnp.float32,
        )
        combined = term if combined is None else combined + term
    activated = jax.nn.gelu(combined, approximate=True).astype(jnp.bfloat16)
    out_ref[...] = jnp.dot(activated, mix_ref[...], preferred_element_type=jnp.float32).astype(
        out_ref.dtype
    )


def shards(fields, coeffs, entries, band_info, conv_weight, mix_weight):
    band_index = lax.axis_index("lat")
    grid_rows = LAT_DEV * lax.axis_size("lat")
    nrows, nlon, members, channels = fields.shape
    coupling = band_coupling(entries, band_info, coeffs, band_index, grid_rows)
    coupling = coupling.astype(jnp.bfloat16).astype(jnp.float32)
    rows = gather_rows(fields)
    rows_in, ext = rows.shape[0], rows.shape[1]
    nwin = -(-nlon // WINDOW)
    depth_rows = (nwin - 1) * WINDOW * ROW_PAD + DEPTH
    rows = jnp.transpose(rows, (1, 0, 2, 3)).reshape(ext * rows_in, members * channels)
    rows = jnp.pad(rows, ((0, depth_rows - ext * rows_in), (0, 0)))
    out_rows = members * nwin * LAT_DEV * LON_PAD
    mixed = pl.pallas_call(
        conv_mix_kernel,
        out_shape=jax.ShapeDtypeStruct((out_rows, CHANNELS), jnp.bfloat16),
        in_specs=[pl.BlockSpec(memory_space=pltpu.VMEM)] * 4,
        out_specs=pl.BlockSpec(memory_space=pltpu.VMEM),
        scratch_shapes=[pltpu.VMEM((BASIS * LAT_DEV * LON_PAD, DEPTH), jnp.bfloat16)],
        cost_estimate=pl.CostEstimate(
            flops=2 * BASIS * LAT_DEV * LON_PAD * DEPTH * 1024 * nwin
            + 2 * out_rows * CHANNELS * CHANNELS * (BASIS + 1),
            transcendentals=out_rows * CHANNELS,
            bytes_accessed=rows.size * 2 + (BASIS + 2) * CHANNELS * CHANNELS * 2,
        ),
    )(coupling, rows, conv_weight, mix_weight)
    mixed = mixed.reshape(members, nwin, LAT_DEV, LON_PAD, CHANNELS)
    mixed = jnp.transpose(mixed, (2, 1, 3, 0, 4)).reshape(LAT_DEV, nwin * LON_PAD, members, CHANNELS)
    return mixed[:, :nlon]


def solution(mesh):
    in_specs = (P("lat", "lon", None, None), P(), P(), P(), P(), P())
    out_specs = P("lat", "lon", None, None)
    return jax.shard_map(shards, mesh=mesh, in_specs=in_specs, out_specs=out_specs, check_vma=False)
```

```python
import jax
import jax.numpy as jnp
from jax import lax
from jax.experimental import pallas as pl
from jax.experimental.pallas import tpu as pltpu
from jax.sharding import PartitionSpec as P

CHANNELS = 512
BASIS = 3
SHIFTS = 7
OVERHANG = 3
LAT_DEV = 4
PIECE_LANES = 32


def band_coupling(entries, band_meta, coeffs, band_index, grid_rows):
    nbands = entries.shape[0]
    blocks = entries.shape[1]
    ids = band_index + jnp.arange(-1, 2, dtype=jnp.int32)
    known = (ids >= 0) & (ids < nbands)
    clamped = jnp.clip(ids, 0, nbands - 1)
    listed = jnp.take(entries, clamped, axis=0)
    meta = jnp.take(band_meta, clamped, axis=0)
    out_rows = listed[:, :, 0, :]
    in_rows = listed[:, :, 1, :]
    shifts = listed[:, :, 2, :]
    filter_rows = listed[:, :, 3, :]
    block_ids = jnp.arange(blocks, dtype=jnp.int32)[None, :, None]
    own_rel = out_rows - clamped[:, None, None] * LAT_DEV
    usable = known[:, None, None] & (block_ids < meta[:, 0, None, None])
    usable = usable & (own_rel >= -meta[:, 1, None, None])
    usable = usable & (own_rel < LAT_DEV + meta[:, 2, None, None])
    usable = usable & (out_rows >= 0) & (out_rows < grid_rows)
    band_start = band_index * LAT_DEV
    rows_in = LAT_DEV + 2 * OVERHANG
    q = out_rows - band_start
    r = in_rows - (band_start - OVERHANG)
    usable = usable & (q >= 0) & (q < LAT_DEV) & (r >= 0) & (r < rows_in)
    piece = (r >= OVERHANG).astype(jnp.int32) + (r >= OVERHANG + LAT_DEV).astype(jnp.int32)
    width = jnp.where(piece == 1, LAT_DEV, OVERHANG)
    local = r - jnp.where(piece == 0, 0, jnp.where(piece == 1, OVERHANG, OVERHANG + LAT_DEV))
    lane = q * 128 + piece * PIECE_LANES + (SHIFTS - 1 - shifts) * width + local
    slot = jnp.where(usable, lane, -1).reshape(-1)
    nslots = LAT_DEV * 128
    slot_hit = (slot[:, None] == jnp.arange(nslots, dtype=jnp.int32)[None, :]).astype(jnp.bfloat16)
    nfilters = coeffs.shape[0]
    filter_hit = (
        filter_rows.reshape(-1)[:, None] == jnp.arange(nfilters, dtype=jnp.int32)[None, :]
    ).astype(jnp.bfloat16)
    counts = lax.dot_general(
        filter_hit, slot_hit, (((0,), (0,)), ((), ())), preferred_element_type=jnp.float32
    )
    coupling = jnp.dot(
        coeffs.T, counts, precision=lax.Precision.HIGHEST, preferred_element_type=jnp.float32
    )
    return coupling


def lon_major(rows):
    count, nlon, members, channels = rows.shape
    return jnp.transpose(rows, (1, 0, 2, 3)).reshape(nlon * count, members * channels)


def gather_pieces(x):
    nlat = lax.axis_size("lat")
    nlon = lax.axis_size("lon")
    lo = SHIFTS - 1

    def move(value, dlat, dlon):
        pairs = []
        for b in range(nlat):
            if 0 <= b + dlat < nlat:
                for j in range(nlon):
                    pairs.append((b * nlon + j, (b + dlat) * nlon + (j + dlon) % nlon))
        return lax.ppermute(value, ("lat", "lon"), pairs)

    own = lon_major(x)
    send_up = lon_major(x[LAT_DEV - OVERHANG :])
    send_down = lon_major(x[:OVERHANG])
    ntail = lo * OVERHANG
    below = move(send_up, 1, 0)
    above = move(send_down, -1, 0)
    left = move(own[own.shape[0] - lo * LAT_DEV :], 0, 1)
    below_left = move(send_up[send_up.shape[0] - ntail :], 1, 1)
    above_left = move(send_down[send_down.shape[0] - ntail :], -1, 1)
    return (
        jnp.concatenate([below_left, below], axis=0),
        jnp.concatenate([left, own], axis=0),
        jnp.concatenate([above_left, above], axis=0),
    )


WINDOW = 32
LON_PAD = 32
TAPS = 128
WIDTHS = (OVERHANG, LAT_DEV, OVERHANG)
DEPTHS = (128, 256, 128)


def conv_mix_kernel(coupling_ref, below_ref, own_ref, above_ref, weight_ref, mix_ref, out_ref, *toeplitz_refs):
    for p in range(3):
        width, depth = WIDTHS[p], DEPTHS[p]
        lane = lax.broadcasted_iota(jnp.int32, (1, TAPS), 1)
        for k in range(BASIS):
            for q in range(LAT_DEV):
                taps = coupling_ref[k : k + 1, q * TAPS : (q + 1) * TAPS]
                if p:
                    taps = pltpu.roll(taps, TAPS - p * PIECE_LANES, 1)
                taps = jnp.where(lane < SHIFTS * width, taps, 0.0)
                if depth > TAPS:
                    taps = jnp.concatenate([taps, jnp.zeros((1, depth - TAPS), jnp.float32)], axis=1)
                for g in range(LON_PAD // 8):
                    block = jnp.broadcast_to(taps, (8, depth))
                    if g:
                        block = pltpu.roll(block, 8 * g * width, 1)
                    block = pltpu.roll(block, 0, 1, stride=width, stride_axis=0)
                    toeplitz_refs[p][pl.ds((k * LAT_DEV + q) * LON_PAD + 8 * g, 8), :] = block.astype(
                        jnp.bfloat16
                    )
    nwin = out_ref.shape[0] // (2 * LAT_DEV * LON_PAD)
    span = LAT_DEV * LON_PAD
    pieces = [[[] for _ in range(2)] for _ in range(BASIS)]
    row_refs = (below_ref, own_ref, above_ref)
    for j in range(nwin):
        conv = None
        for p in range(3):
            window = row_refs[p][pl.ds(j * WINDOW * WIDTHS[p], DEPTHS[p]), :]
            term = jnp.dot(toeplitz_refs[p][...], window, preferred_element_type=jnp.float32)
            conv = term if conv is None else conv + term
        for k in range(BASIS):
            for m in range(2):
                pieces[k][m].append(conv[k * span : (k + 1) * span, m * CHANNELS : (m + 1) * CHANNELS])
    combined = None
    for k in range(BASIS):
        features = jnp.concatenate(pieces[k][0] + pieces[k][1], axis=0).astype(jnp.bfloat16)
        term = jnp.dot(
            features,
            weight_ref[k * CHANNELS : (k + 1) * CHANNELS, :],
            preferred_element_type=jnp.float32,
        )
        combined = term if combined is None else combined + term
    activated = jax.nn.gelu(combined, approximate=True).astype(jnp.bfloat16)
    out_ref[...] = jnp.dot(activated, mix_ref[...], preferred_element_type=jnp.float32).astype(
        out_ref.dtype
    )


def shards(fields, coeffs, entries, band_info, conv_weight, mix_weight):
    band_index = lax.axis_index("lat")
    grid_rows = LAT_DEV * lax.axis_size("lat")
    nrows, nlon, members, channels = fields.shape
    coupling = band_coupling(entries, band_info, coeffs, band_index, grid_rows)
    coupling = coupling.astype(jnp.bfloat16).astype(jnp.float32)
    nwin = -(-nlon // WINDOW)
    pieces = []
    for piece, width, depth in zip(gather_pieces(fields), WIDTHS, DEPTHS):
        need = (nwin - 1) * WINDOW * width + depth
        pieces.append(jnp.pad(piece, ((0, need - piece.shape[0]), (0, 0))))
    out_rows = members * nwin * LAT_DEV * LON_PAD
    toeplitz_rows = BASIS * LAT_DEV * LON_PAD
    mixed = pl.pallas_call(
        conv_mix_kernel,
        out_shape=jax.ShapeDtypeStruct((out_rows, CHANNELS), jnp.bfloat16),
        in_specs=[pl.BlockSpec(memory_space=pltpu.VMEM)] * 6,
        out_specs=pl.BlockSpec(memory_space=pltpu.VMEM),
        scratch_shapes=[pltpu.VMEM((toeplitz_rows, depth), jnp.bfloat16) for depth in DEPTHS],
        cost_estimate=pl.CostEstimate(
            flops=2 * toeplitz_rows * sum(DEPTHS) * 1024 * nwin
            + 2 * out_rows * CHANNELS * CHANNELS * (BASIS + 1),
            transcendentals=out_rows * CHANNELS,
            bytes_accessed=sum(p.size for p in pieces) * 2 + (BASIS + 2) * CHANNELS * CHANNELS * 2,
        ),
    )(coupling, *pieces, conv_weight, mix_weight)
    mixed = mixed.reshape(members, nwin, LAT_DEV, LON_PAD, CHANNELS)
    mixed = jnp.transpose(mixed, (2, 1, 3, 0, 4)).reshape(LAT_DEV, nwin * LON_PAD, members, CHANNELS)
    return mixed[:, :nlon]


def solution(mesh):
    in_specs = (P("lat", "lon", None, None), P(), P(), P(), P(), P())
    out_specs = P("lat", "lon", None, None)
    return jax.shard_map(shards, mesh=mesh, in_specs=in_specs, out_specs=out_specs, check_vma=False)
```

```python
import jax
import jax.numpy as jnp
from jax import lax
from jax.experimental import pallas as pl
from jax.experimental.pallas import tpu as pltpu
from jax.sharding import PartitionSpec as P

CHANNELS = 512
BASIS = 3
SHIFTS = 7
OVERHANG = 3
LAT_DEV = 4
PIECE_LANES = 32


def band_coupling(entries, band_meta, coeffs, band_index, grid_rows):
    nbands = entries.shape[0]
    blocks = entries.shape[1]
    ids = band_index + jnp.arange(-1, 2, dtype=jnp.int32)
    known = (ids >= 0) & (ids < nbands)
    clamped = jnp.clip(ids, 0, nbands - 1)
    listed = jnp.take(entries, clamped, axis=0)
    meta = jnp.take(band_meta, clamped, axis=0)
    out_rows = listed[:, :, 0, :]
    in_rows = listed[:, :, 1, :]
    shifts = listed[:, :, 2, :]
    filter_rows = listed[:, :, 3, :]
    block_ids = jnp.arange(blocks, dtype=jnp.int32)[None, :, None]
    own_rel = out_rows - clamped[:, None, None] * LAT_DEV
    usable = known[:, None, None] & (block_ids < meta[:, 0, None, None])
    usable = usable & (own_rel >= -meta[:, 1, None, None])
    usable = usable & (own_rel < LAT_DEV + meta[:, 2, None, None])
    usable = usable & (out_rows >= 0) & (out_rows < grid_rows)
    band_start = band_index * LAT_DEV
    rows_in = LAT_DEV + 2 * OVERHANG
    q = out_rows - band_start
    r = in_rows - (band_start - OVERHANG)
    usable = usable & (q >= 0) & (q < LAT_DEV) & (r >= 0) & (r < rows_in)
    piece = (r >= OVERHANG).astype(jnp.int32) + (r >= OVERHANG + LAT_DEV).astype(jnp.int32)
    width = jnp.where(piece == 1, LAT_DEV, OVERHANG)
    local = r - jnp.where(piece == 0, 0, jnp.where(piece == 1, OVERHANG, OVERHANG + LAT_DEV))
    lane = q * 128 + piece * PIECE_LANES + (SHIFTS - 1 - shifts) * width + local
    slot = jnp.where(usable, lane, -1).reshape(-1)
    nslots = LAT_DEV * 128
    slot_hit = (slot[:, None] == jnp.arange(nslots, dtype=jnp.int32)[None, :]).astype(jnp.bfloat16)
    nfilters = coeffs.shape[0]
    filter_hit = (
        filter_rows.reshape(-1)[:, None] == jnp.arange(nfilters, dtype=jnp.int32)[None, :]
    ).astype(jnp.bfloat16)
    counts = lax.dot_general(
        filter_hit, slot_hit, (((0,), (0,)), ((), ())), preferred_element_type=jnp.float32
    )
    coupling = jnp.dot(
        coeffs.T, counts, precision=lax.Precision.HIGHEST, preferred_element_type=jnp.float32
    )
    return coupling


def lon_major(rows):
    count, nlon, members, channels = rows.shape
    return jnp.transpose(rows, (1, 0, 2, 3)).reshape(nlon * count, members * channels)


def gather_pieces(x):
    nlat = lax.axis_size("lat")
    nlon = lax.axis_size("lon")
    lo = SHIFTS - 1
    left = lax.ppermute(x[:, x.shape[1] - lo :], "lon", [(j, (j + 1) % nlon) for j in range(nlon)])
    ext = jnp.concatenate([left, x], axis=1)
    down = [(b, b + 1) for b in range(nlat - 1)]
    below = lax.ppermute(ext[LAT_DEV - OVERHANG :], "lat", down)
    above = lax.ppermute(ext[:OVERHANG], "lat", [(t, s) for s, t in down])
    return lon_major(below), lon_major(ext), lon_major(above)


WINDOW = 32
LON_PAD = 32
TAPS = 128
WIDTHS = (OVERHANG, LAT_DEV, OVERHANG)
DEPTHS = (128, 256, 128)


def conv_mix_kernel(coupling_ref, below_ref, own_ref, above_ref, weight_ref, mix_ref, out_ref, *toeplitz_refs):
    for p in range(3):
        width, depth = WIDTHS[p], DEPTHS[p]
        lane = lax.broadcasted_iota(jnp.int32, (1, TAPS), 1)
        for k in range(BASIS):
            for q in range(LAT_DEV):
                taps = coupling_ref[k : k + 1, q * TAPS : (q + 1) * TAPS]
                if p:
                    taps = pltpu.roll(taps, TAPS - p * PIECE_LANES, 1)
                taps = jnp.where(lane < SHIFTS * width, taps, 0.0)
                if depth > TAPS:
                    taps = jnp.concatenate([taps, jnp.zeros((1, depth - TAPS), jnp.float32)], axis=1)
                for g in range(LON_PAD // 8):
                    block = jnp.broadcast_to(taps, (8, depth))
                    if g:
                        block = pltpu.roll(block, 8 * g * width, 1)
                    block = pltpu.roll(block, 0, 1, stride=width, stride_axis=0)
                    toeplitz_refs[p][pl.ds((k * LAT_DEV + q) * LON_PAD + 8 * g, 8), :] = block.astype(
                        jnp.bfloat16
                    )
    nwin = out_ref.shape[0] // (2 * LAT_DEV * LON_PAD)
    span = LAT_DEV * LON_PAD
    pieces = [[[] for _ in range(2)] for _ in range(BASIS)]
    row_refs = (below_ref, own_ref, above_ref)
    for j in range(nwin):
        conv = None
        for p in range(3):
            window = row_refs[p][pl.ds(j * WINDOW * WIDTHS[p], DEPTHS[p]), :]
            term = jnp.dot(toeplitz_refs[p][...], window, preferred_element_type=jnp.float32)
            conv = term if conv is None else conv + term
        for k in range(BASIS):
            for m in range(2):
                pieces[k][m].append(conv[k * span : (k + 1) * span, m * CHANNELS : (m + 1) * CHANNELS])
    combined = None
    for k in range(BASIS):
        features = jnp.concatenate(pieces[k][0] + pieces[k][1], axis=0).astype(jnp.bfloat16)
        term = jnp.dot(
            features,
            weight_ref[k * CHANNELS : (k + 1) * CHANNELS, :],
            preferred_element_type=jnp.float32,
        )
        combined = term if combined is None else combined + term
    activated = jax.nn.gelu(combined, approximate=True).astype(jnp.bfloat16)
    out_ref[...] = jnp.dot(activated, mix_ref[...], preferred_element_type=jnp.float32).astype(
        out_ref.dtype
    )


def shards(fields, coeffs, entries, band_info, conv_weight, mix_weight):
    band_index = lax.axis_index("lat")
    grid_rows = LAT_DEV * lax.axis_size("lat")
    nrows, nlon, members, channels = fields.shape
    coupling = band_coupling(entries, band_info, coeffs, band_index, grid_rows)
    coupling = coupling.astype(jnp.bfloat16).astype(jnp.float32)
    nwin = -(-nlon // WINDOW)
    pieces = []
    for piece, width, depth in zip(gather_pieces(fields), WIDTHS, DEPTHS):
        need = (nwin - 1) * WINDOW * width + depth
        pieces.append(jnp.pad(piece, ((0, need - piece.shape[0]), (0, 0))))
    out_rows = members * nwin * LAT_DEV * LON_PAD
    toeplitz_rows = BASIS * LAT_DEV * LON_PAD
    mixed = pl.pallas_call(
        conv_mix_kernel,
        out_shape=jax.ShapeDtypeStruct((out_rows, CHANNELS), jnp.bfloat16),
        in_specs=[pl.BlockSpec(memory_space=pltpu.VMEM)] * 6,
        out_specs=pl.BlockSpec(memory_space=pltpu.VMEM),
        scratch_shapes=[pltpu.VMEM((toeplitz_rows, depth), jnp.bfloat16) for depth in DEPTHS],
        cost_estimate=pl.CostEstimate(
            flops=2 * toeplitz_rows * sum(DEPTHS) * 1024 * nwin
            + 2 * out_rows * CHANNELS * CHANNELS * (BASIS + 1),
            transcendentals=out_rows * CHANNELS,
            bytes_accessed=sum(p.size for p in pieces) * 2 + (BASIS + 2) * CHANNELS * CHANNELS * 2,
        ),
    )(coupling, *pieces, conv_weight, mix_weight)
    mixed = mixed.reshape(members, nwin, LAT_DEV, LON_PAD, CHANNELS)
    mixed = jnp.transpose(mixed, (2, 1, 3, 0, 4)).reshape(LAT_DEV, nwin * LON_PAD, members, CHANNELS)
    return mixed[:, :nlon]


def solution(mesh):
    in_specs = (P("lat", "lon", None, None), P(), P(), P(), P(), P())
    out_specs = P("lat", "lon", None, None)
    return jax.shard_map(shards, mesh=mesh, in_specs=in_specs, out_specs=out_specs, check_vma=False)
```

```python
import jax
import jax.numpy as jnp
from jax import lax
from jax.experimental import pallas as pl
from jax.experimental.pallas import tpu as pltpu
from jax.sharding import PartitionSpec as P

CHANNELS = 512
BASIS = 3
SHIFTS = 7
OVERHANG = 3
LAT_DEV = 4
PIECE_LANES = 32


def band_coupling(entries, band_meta, coeffs, band_index, grid_rows):
    nbands = entries.shape[0]
    blocks = entries.shape[1]
    ids = band_index + jnp.arange(-1, 2, dtype=jnp.int32)
    known = (ids >= 0) & (ids < nbands)
    clamped = jnp.clip(ids, 0, nbands - 1)
    listed = jnp.take(entries, clamped, axis=0)
    meta = jnp.take(band_meta, clamped, axis=0)
    out_rows = listed[:, :, 0, :]
    in_rows = listed[:, :, 1, :]
    shifts = listed[:, :, 2, :]
    filter_rows = listed[:, :, 3, :]
    block_ids = jnp.arange(blocks, dtype=jnp.int32)[None, :, None]
    own_rel = out_rows - clamped[:, None, None] * LAT_DEV
    usable = known[:, None, None] & (block_ids < meta[:, 0, None, None])
    usable = usable & (own_rel >= -meta[:, 1, None, None])
    usable = usable & (own_rel < LAT_DEV + meta[:, 2, None, None])
    usable = usable & (out_rows >= 0) & (out_rows < grid_rows)
    band_start = band_index * LAT_DEV
    rows_in = LAT_DEV + 2 * OVERHANG
    q = out_rows - band_start
    r = in_rows - (band_start - OVERHANG)
    usable = usable & (q >= 0) & (q < LAT_DEV) & (r >= 0) & (r < rows_in)
    piece = (r >= OVERHANG).astype(jnp.int32) + (r >= OVERHANG + LAT_DEV).astype(jnp.int32)
    width = jnp.where(piece == 1, LAT_DEV, OVERHANG)
    local = r - jnp.where(piece == 0, 0, jnp.where(piece == 1, OVERHANG, OVERHANG + LAT_DEV))
    lane = q * 128 + piece * PIECE_LANES + (SHIFTS - 1 - shifts) * width + local
    slot = jnp.where(usable, lane, -1).reshape(-1)
    nslots = LAT_DEV * 128
    slot_hit = (slot[:, None] == jnp.arange(nslots, dtype=jnp.int32)[None, :]).astype(jnp.bfloat16)
    nfilters = coeffs.shape[0]
    filter_hit = (
        filter_rows.reshape(-1)[:, None] == jnp.arange(nfilters, dtype=jnp.int32)[None, :]
    ).astype(jnp.bfloat16)
    counts = lax.dot_general(
        filter_hit, slot_hit, (((0,), (0,)), ((), ())), preferred_element_type=jnp.float32
    )
    coupling = jnp.dot(
        coeffs.T, counts, precision=lax.Precision.HIGHEST, preferred_element_type=jnp.float32
    )
    return coupling


def lon_major(rows):
    count, nlon, members, channels = rows.shape
    return jnp.transpose(rows, (1, 0, 2, 3)).reshape(nlon * count, members * channels)


def gather_pieces(x):
    nlat = lax.axis_size("lat")
    nlon = lax.axis_size("lon")
    lo = SHIFTS - 1
    tail = x[:, x.shape[1] - lo :]

    def move(value, dlat, dlon):
        pairs = []
        for b in range(nlat):
            if 0 <= b + dlat < nlat:
                for j in range(nlon):
                    pairs.append((b * nlon + j, (b + dlat) * nlon + (j + dlon) % nlon))
        return lax.ppermute(value, ("lat", "lon"), pairs)

    below = move(x[LAT_DEV - OVERHANG :], 1, 0)
    above = move(x[:OVERHANG], -1, 0)
    below_left = move(tail[LAT_DEV - OVERHANG :], 1, 1)
    above_left = move(tail[:OVERHANG], -1, 1)
    left = move(tail, 0, 1)
    return (
        lon_major(jnp.concatenate([below_left, below], axis=1)),
        lon_major(jnp.concatenate([left, x], axis=1)),
        lon_major(jnp.concatenate([above_left, above], axis=1)),
    )


WINDOW = 32
LON_PAD = 32
TAPS = 128
WIDTHS = (OVERHANG, LAT_DEV, OVERHANG)
DEPTHS = (128, 256, 128)


def conv_mix_kernel(coupling_ref, below_ref, own_ref, above_ref, weight_ref, mix_ref, out_ref, *toeplitz_refs):
    for p in range(3):
        width, depth = WIDTHS[p], DEPTHS[p]
        lane = lax.broadcasted_iota(jnp.int32, (1, TAPS), 1)
        for k in range(BASIS):
            for q in range(LAT_DEV):
                taps = coupling_ref[k : k + 1, q * TAPS : (q + 1) * TAPS]
                if p:
                    taps = pltpu.roll(taps, TAPS - p * PIECE_LANES, 1)
                taps = jnp.where(lane < SHIFTS * width, taps, 0.0)
                if depth > TAPS:
                    taps = jnp.concatenate([taps, jnp.zeros((1, depth - TAPS), jnp.float32)], axis=1)
                for g in range(LON_PAD // 8):
                    block = jnp.broadcast_to(taps, (8, depth))
                    if g:
                        block = pltpu.roll(block, 8 * g * width, 1)
                    block = pltpu.roll(block, 0, 1, stride=width, stride_axis=0)
                    toeplitz_refs[p][pl.ds((k * LAT_DEV + q) * LON_PAD + 8 * g, 8), :] = block.astype(
                        jnp.bfloat16
                    )
    nwin = out_ref.shape[0] // (2 * LAT_DEV * LON_PAD)
    span = LAT_DEV * LON_PAD
    pieces = [[[] for _ in range(2)] for _ in range(BASIS)]
    row_refs = (below_ref, own_ref, above_ref)
    for j in range(nwin):
        conv = None
        for p in range(3):
            window = row_refs[p][pl.ds(j * WINDOW * WIDTHS[p], DEPTHS[p]), :]
            term = jnp.dot(toeplitz_refs[p][...], window, preferred_element_type=jnp.float32)
            conv = term if conv is None else conv + term
        for k in range(BASIS):
            for m in range(2):
                pieces[k][m].append(conv[k * span : (k + 1) * span, m * CHANNELS : (m + 1) * CHANNELS])
    combined = None
    for k in range(BASIS):
        features = jnp.concatenate(pieces[k][0] + pieces[k][1], axis=0).astype(jnp.bfloat16)
        term = jnp.dot(
            features,
            weight_ref[k * CHANNELS : (k + 1) * CHANNELS, :],
            preferred_element_type=jnp.float32,
        )
        combined = term if combined is None else combined + term
    activated = jax.nn.gelu(combined, approximate=True).astype(jnp.bfloat16)
    out_ref[...] = jnp.dot(activated, mix_ref[...], preferred_element_type=jnp.float32).astype(
        out_ref.dtype
    )


def shards(fields, coeffs, entries, band_info, conv_weight, mix_weight):
    band_index = lax.axis_index("lat")
    grid_rows = LAT_DEV * lax.axis_size("lat")
    nrows, nlon, members, channels = fields.shape
    coupling = band_coupling(entries, band_info, coeffs, band_index, grid_rows)
    coupling = coupling.astype(jnp.bfloat16).astype(jnp.float32)
    nwin = -(-nlon // WINDOW)
    pieces = []
    for piece, width, depth in zip(gather_pieces(fields), WIDTHS, DEPTHS):
        need = (nwin - 1) * WINDOW * width + depth
        pieces.append(jnp.pad(piece, ((0, need - piece.shape[0]), (0, 0))))
    out_rows = members * nwin * LAT_DEV * LON_PAD
    toeplitz_rows = BASIS * LAT_DEV * LON_PAD
    mixed = pl.pallas_call(
        conv_mix_kernel,
        out_shape=jax.ShapeDtypeStruct((out_rows, CHANNELS), jnp.bfloat16),
        in_specs=[pl.BlockSpec(memory_space=pltpu.VMEM)] * 6,
        out_specs=pl.BlockSpec(memory_space=pltpu.VMEM),
        scratch_shapes=[pltpu.VMEM((toeplitz_rows, depth), jnp.bfloat16) for depth in DEPTHS],
        cost_estimate=pl.CostEstimate(
            flops=2 * toeplitz_rows * sum(DEPTHS) * 1024 * nwin
            + 2 * out_rows * CHANNELS * CHANNELS * (BASIS + 1),
            transcendentals=out_rows * CHANNELS,
            bytes_accessed=sum(p.size for p in pieces) * 2 + (BASIS + 2) * CHANNELS * CHANNELS * 2,
        ),
    )(coupling, *pieces, conv_weight, mix_weight)
    mixed = mixed.reshape(members, nwin, LAT_DEV, LON_PAD, CHANNELS)
    mixed = jnp.transpose(mixed, (2, 1, 3, 0, 4)).reshape(LAT_DEV, nwin * LON_PAD, members, CHANNELS)
    return mixed[:, :nlon]


def solution(mesh):
    in_specs = (P("lat", "lon", None, None), P(), P(), P(), P(), P())
    out_specs = P("lat", "lon", None, None)
    return jax.shard_map(shards, mesh=mesh, in_specs=in_specs, out_specs=out_specs, check_vma=False)
```

```python
import jax
import jax.numpy as jnp
from jax import lax
from jax.experimental import pallas as pl
from jax.experimental.pallas import tpu as pltpu
from jax.sharding import PartitionSpec as P

CHANNELS = 512
BASIS = 3
SHIFTS = 7
OVERHANG = 3
LAT_DEV = 4
PIECE_LANES = 32


def band_coupling(entries, band_meta, coeffs, band_index, grid_rows):
    nbands = entries.shape[0]
    blocks = entries.shape[1]
    ids = band_index + jnp.arange(-1, 2, dtype=jnp.int32)
    known = (ids >= 0) & (ids < nbands)
    clamped = jnp.clip(ids, 0, nbands - 1)
    listed = jnp.take(entries, clamped, axis=0)
    meta = jnp.take(band_meta, clamped, axis=0)
    out_rows = listed[:, :, 0, :]
    in_rows = listed[:, :, 1, :]
    shifts = listed[:, :, 2, :]
    filter_rows = listed[:, :, 3, :]
    block_ids = jnp.arange(blocks, dtype=jnp.int32)[None, :, None]
    own_rel = out_rows - clamped[:, None, None] * LAT_DEV
    usable = known[:, None, None] & (block_ids < meta[:, 0, None, None])
    usable = usable & (own_rel >= -meta[:, 1, None, None])
    usable = usable & (own_rel < LAT_DEV + meta[:, 2, None, None])
    usable = usable & (out_rows >= 0) & (out_rows < grid_rows)
    band_start = band_index * LAT_DEV
    rows_in = LAT_DEV + 2 * OVERHANG
    q = out_rows - band_start
    r = in_rows - (band_start - OVERHANG)
    usable = usable & (q >= 0) & (q < LAT_DEV) & (r >= 0) & (r < rows_in)
    piece = (r >= OVERHANG).astype(jnp.int32) + (r >= OVERHANG + LAT_DEV).astype(jnp.int32)
    width = jnp.where(piece == 1, LAT_DEV, OVERHANG)
    local = r - jnp.where(piece == 0, 0, jnp.where(piece == 1, OVERHANG, OVERHANG + LAT_DEV))
    lane = q * 128 + piece * PIECE_LANES + (SHIFTS - 1 - shifts) * width + local
    slot = jnp.where(usable, lane, -1).reshape(-1)
    nslots = LAT_DEV * 128
    slot_hit = (slot[:, None] == jnp.arange(nslots, dtype=jnp.int32)[None, :]).astype(jnp.bfloat16)
    nfilters = coeffs.shape[0]
    filter_hit = (
        filter_rows.reshape(-1)[:, None] == jnp.arange(nfilters, dtype=jnp.int32)[None, :]
    ).astype(jnp.bfloat16)
    counts = lax.dot_general(
        filter_hit, slot_hit, (((0,), (0,)), ((), ())), preferred_element_type=jnp.float32
    )
    coupling = jnp.dot(
        coeffs.T, counts, precision=lax.Precision.HIGHEST, preferred_element_type=jnp.float32
    )
    return coupling


def lon_major(rows):
    count, nlon, members, channels = rows.shape
    return jnp.transpose(rows, (1, 0, 2, 3)).reshape(nlon * count, members * channels)


def gather_pieces(x):
    nlat = lax.axis_size("lat")
    nlon = lax.axis_size("lon")
    lo = SHIFTS - 1
    tail = x[:, x.shape[1] - lo :]

    def move(value, dlat, dlon):
        pairs = []
        for b in range(nlat):
            if 0 <= b + dlat < nlat:
                for j in range(nlon):
                    pairs.append((b * nlon + j, (b + dlat) * nlon + (j + dlon) % nlon))
        return lax.ppermute(value, ("lat", "lon"), pairs)

    below = move(x[LAT_DEV - OVERHANG :], 1, 0)
    above = move(x[:OVERHANG], -1, 0)
    below_left = move(tail[LAT_DEV - OVERHANG :], 1, 1)
    above_left = move(tail[:OVERHANG], -1, 1)
    left = move(tail, 0, 1)
    return (
        lon_major(jnp.concatenate([below_left, below], axis=1)),
        lon_major(jnp.concatenate([left, x], axis=1)),
        lon_major(jnp.concatenate([above_left, above], axis=1)),
    )


WINDOW = 32
LON_PAD = 32
TAPS = 128
WIDTHS = (OVERHANG, LAT_DEV, OVERHANG)
DEPTHS = (128, 256, 128)


def conv_mix_kernel(
    coupling_ref, below_ref, own_ref, above_ref, weight_ref, mix_ref, out_ref, feature_ref, *toeplitz_refs
):
    for p in range(3):
        width, depth = WIDTHS[p], DEPTHS[p]
        lane = lax.broadcasted_iota(jnp.int32, (1, TAPS), 1)
        for k in range(BASIS):
            for q in range(LAT_DEV):
                taps = coupling_ref[k : k + 1, q * TAPS : (q + 1) * TAPS]
                if p:
                    taps = pltpu.roll(taps, TAPS - p * PIECE_LANES, 1)
                taps = jnp.where(lane < SHIFTS * width, taps, 0.0)
                if depth > TAPS:
                    taps = jnp.concatenate([taps, jnp.zeros((1, depth - TAPS), jnp.float32)], axis=1)
                for g in range(LON_PAD // 8):
                    block = jnp.broadcast_to(taps, (8, depth))
                    if g:
                        block = pltpu.roll(block, 8 * g * width, 1)
                    block = pltpu.roll(block, 0, 1, stride=width, stride_axis=0)
                    toeplitz_refs[p][pl.ds((k * LAT_DEV + q) * LON_PAD + 8 * g, 8), :] = block.astype(
                        jnp.bfloat16
                    )
    nwin = out_ref.shape[0] // (2 * LAT_DEV * LON_PAD)
    row_refs = (below_ref, own_ref, above_ref)
    for j in range(nwin):
        conv = None
        for p in range(3):
            window = row_refs[p][pl.ds(j * WINDOW * WIDTHS[p], DEPTHS[p]), :]
            term = jnp.dot(toeplitz_refs[p][...], window, preferred_element_type=jnp.float32)
            conv = term if conv is None else conv + term
        for k in range(BASIS):
            for q in range(LAT_DEV):
                block = conv[(k * LAT_DEV + q) * LON_PAD : (k * LAT_DEV + q + 1) * LON_PAD]
                base = (q * nwin + j) * LON_PAD * 2
                for m in range(2):
                    for c in range(CHANNELS // 128):
                        lanes = m * CHANNELS + c * 128
                        feature_ref[k * (CHANNELS // 128) + c, pl.ds(base + m, LON_PAD, stride=2), :] = (
                            block[:, lanes : lanes + 128]
                        )
    combined = None
    for k in range(BASIS):
        features = jnp.concatenate(
            [feature_ref[k * (CHANNELS // 128) + c] for c in range(CHANNELS // 128)], axis=1
        ).astype(jnp.bfloat16)
        term = jnp.dot(
            features,
            weight_ref[k * CHANNELS : (k + 1) * CHANNELS, :],
            preferred_element_type=jnp.float32,
        )
        combined = term if combined is None else combined + term
    activated = jax.nn.gelu(combined, approximate=True).astype(jnp.bfloat16)
    out_ref[...] = jnp.dot(activated, mix_ref[...], preferred_element_type=jnp.float32).astype(
        out_ref.dtype
    )


def shards(fields, coeffs, entries, band_info, conv_weight, mix_weight):
    band_index = lax.axis_index("lat")
    grid_rows = LAT_DEV * lax.axis_size("lat")
    nrows, nlon, members, channels = fields.shape
    coupling = band_coupling(entries, band_info, coeffs, band_index, grid_rows)
    coupling = coupling.astype(jnp.bfloat16).astype(jnp.float32)
    nwin = -(-nlon // WINDOW)
    pieces = []
    for piece, width, depth in zip(gather_pieces(fields), WIDTHS, DEPTHS):
        need = (nwin - 1) * WINDOW * width + depth
        pieces.append(jnp.pad(piece, ((0, need - piece.shape[0]), (0, 0))))
    out_rows = members * nwin * LAT_DEV * LON_PAD
    toeplitz_rows = BASIS * LAT_DEV * LON_PAD
    mixed = pl.pallas_call(
        conv_mix_kernel,
        out_shape=jax.ShapeDtypeStruct((out_rows, CHANNELS), jnp.bfloat16),
        in_specs=[pl.BlockSpec(memory_space=pltpu.VMEM)] * 6,
        out_specs=pl.BlockSpec(memory_space=pltpu.VMEM),
        scratch_shapes=[pltpu.VMEM((BASIS * CHANNELS // 128, out_rows, 128), jnp.float32)]
        + [pltpu.VMEM((toeplitz_rows, depth), jnp.bfloat16) for depth in DEPTHS],
        cost_estimate=pl.CostEstimate(
            flops=2 * toeplitz_rows * sum(DEPTHS) * 1024 * nwin
            + 2 * out_rows * CHANNELS * CHANNELS * (BASIS + 1),
            transcendentals=out_rows * CHANNELS,
            bytes_accessed=sum(p.size for p in pieces) * 2 + (BASIS + 2) * CHANNELS * CHANNELS * 2,
        ),
    )(coupling, *pieces, conv_weight, mix_weight)
    mixed = mixed.reshape(LAT_DEV, nwin * LON_PAD, members, CHANNELS)
    return mixed[:, :nlon]


def solution(mesh):
    in_specs = (P("lat", "lon", None, None), P(), P(), P(), P(), P())
    out_specs = P("lat", "lon", None, None)
    return jax.shard_map(shards, mesh=mesh, in_specs=in_specs, out_specs=out_specs, check_vma=False)
```

```python
import jax
import jax.numpy as jnp
from jax import lax
from jax.experimental import pallas as pl
from jax.experimental.pallas import tpu as pltpu
from jax.sharding import PartitionSpec as P

CHANNELS = 512
BASIS = 3
SHIFTS = 7
OVERHANG = 3
LAT_DEV = 4
PIECE_LANES = 32


def band_coupling(entries, band_meta, coeffs, band_index, grid_rows):
    nbands = entries.shape[0]
    blocks = entries.shape[1]
    ids = band_index + jnp.arange(-1, 2, dtype=jnp.int32)
    known = (ids >= 0) & (ids < nbands)
    clamped = jnp.clip(ids, 0, nbands - 1)
    listed = jnp.take(entries, clamped, axis=0)
    meta = jnp.take(band_meta, clamped, axis=0)
    out_rows = listed[:, :, 0, :]
    in_rows = listed[:, :, 1, :]
    shifts = listed[:, :, 2, :]
    filter_rows = listed[:, :, 3, :]
    block_ids = jnp.arange(blocks, dtype=jnp.int32)[None, :, None]
    own_rel = out_rows - clamped[:, None, None] * LAT_DEV
    usable = known[:, None, None] & (block_ids < meta[:, 0, None, None])
    usable = usable & (own_rel >= -meta[:, 1, None, None])
    usable = usable & (own_rel < LAT_DEV + meta[:, 2, None, None])
    usable = usable & (out_rows >= 0) & (out_rows < grid_rows)
    band_start = band_index * LAT_DEV
    rows_in = LAT_DEV + 2 * OVERHANG
    q = out_rows - band_start
    r = in_rows - (band_start - OVERHANG)
    usable = usable & (q >= 0) & (q < LAT_DEV) & (r >= 0) & (r < rows_in)
    piece = (r >= OVERHANG).astype(jnp.int32) + (r >= OVERHANG + LAT_DEV).astype(jnp.int32)
    width = jnp.where(piece == 1, LAT_DEV, OVERHANG)
    local = r - jnp.where(piece == 0, 0, jnp.where(piece == 1, OVERHANG, OVERHANG + LAT_DEV))
    lane = q * 128 + piece * PIECE_LANES + (SHIFTS - 1 - shifts) * width + local
    slot = jnp.where(usable, lane, -1).reshape(-1)
    nslots = LAT_DEV * 128
    slot_hit = (slot[:, None] == jnp.arange(nslots, dtype=jnp.int32)[None, :]).astype(jnp.bfloat16)
    nfilters = coeffs.shape[0]
    filter_hit = (
        filter_rows.reshape(-1)[:, None] == jnp.arange(nfilters, dtype=jnp.int32)[None, :]
    ).astype(jnp.bfloat16)
    counts = lax.dot_general(
        filter_hit, slot_hit, (((0,), (0,)), ((), ())), preferred_element_type=jnp.float32
    )
    coupling = jnp.dot(
        coeffs.T, counts, precision=lax.Precision.HIGHEST, preferred_element_type=jnp.float32
    )
    return coupling


def lon_major(rows):
    count, nlon, members, channels = rows.shape
    return jnp.transpose(rows, (1, 0, 2, 3)).reshape(nlon * count, members * channels)


def gather_pieces(x):
    nlat = lax.axis_size("lat")
    nlon = lax.axis_size("lon")
    lo = SHIFTS - 1
    tail = x[:, x.shape[1] - lo :]

    def move(value, dlat, dlon):
        pairs = []
        for b in range(nlat):
            if 0 <= b + dlat < nlat:
                for j in range(nlon):
                    pairs.append((b * nlon + j, (b + dlat) * nlon + (j + dlon) % nlon))
        return lax.ppermute(value, ("lat", "lon"), pairs)

    below = move(x[LAT_DEV - OVERHANG :], 1, 0)
    above = move(x[:OVERHANG], -1, 0)
    below_left = move(tail[LAT_DEV - OVERHANG :], 1, 1)
    above_left = move(tail[:OVERHANG], -1, 1)
    left = move(tail, 0, 1)
    return (
        lon_major(jnp.concatenate([below_left, below], axis=1)),
        lon_major(jnp.concatenate([left, x], axis=1)),
        lon_major(jnp.concatenate([above_left, above], axis=1)),
    )


WINDOW = 32
LON_PAD = 32
TAPS = 128
WIDTHS = (OVERHANG, LAT_DEV, OVERHANG)
DEPTHS = (128, 256, 128)


def conv_mix_kernel(
    coupling_ref, below_ref, own_ref, above_ref, weight_ref, mix_ref, out_ref, feature_ref, *toeplitz_refs
):
    for p in range(3):
        width, depth = WIDTHS[p], DEPTHS[p]
        lane = lax.broadcasted_iota(jnp.int32, (1, TAPS), 1)
        for k in range(BASIS):
            for q in range(LAT_DEV):
                taps = coupling_ref[k : k + 1, q * TAPS : (q + 1) * TAPS]
                if p:
                    taps = pltpu.roll(taps, TAPS - p * PIECE_LANES, 1)
                taps = jnp.where(lane < SHIFTS * width, taps, 0.0)
                if depth > TAPS:
                    taps = jnp.concatenate([taps, jnp.zeros((1, depth - TAPS), jnp.float32)], axis=1)
                for g in range(LON_PAD // 8):
                    block = jnp.broadcast_to(taps, (8, depth))
                    if g:
                        block = pltpu.roll(block, 8 * g * width, 1)
                    block = pltpu.roll(block, 0, 1, stride=width, stride_axis=0)
                    toeplitz_refs[p][pl.ds((k * LAT_DEV + q) * LON_PAD + 8 * g, 8), :] = block.astype(
                        jnp.bfloat16
                    )
    nlon = out_ref.shape[0] // (2 * LAT_DEV)
    nwin = -(-nlon // WINDOW)
    row_refs = (below_ref, own_ref, above_ref)
    for j in range(nwin):
        conv = None
        for p in range(3):
            window = row_refs[p][pl.ds(j * WINDOW * WIDTHS[p], DEPTHS[p]), :]
            term = jnp.dot(toeplitz_refs[p][...], window, preferred_element_type=jnp.float32)
            conv = term if conv is None else conv + term
        for k in range(BASIS):
            for q in range(LAT_DEV):
                count = min(WINDOW, nlon - j * WINDOW)
                first = (k * LAT_DEV + q) * LON_PAD
                block = conv[first : first + count]
                base = (q * nlon + j * WINDOW) * 2
                for m in range(2):
                    for c in range(CHANNELS // 128):
                        lanes = m * CHANNELS + c * 128
                        feature_ref[k * (CHANNELS // 128) + c, pl.ds(base + m, count, stride=2), :] = (
                            block[:, lanes : lanes + 128]
                        )
    combined = None
    for k in range(BASIS):
        features = jnp.concatenate(
            [feature_ref[k * (CHANNELS // 128) + c] for c in range(CHANNELS // 128)], axis=1
        ).astype(jnp.bfloat16)
        term = jnp.dot(
            features,
            weight_ref[k * CHANNELS : (k + 1) * CHANNELS, :],
            preferred_element_type=jnp.float32,
        )
        combined = term if combined is None else combined + term
    activated = jax.nn.gelu(combined, approximate=True).astype(jnp.bfloat16)
    out_ref[...] = jnp.dot(activated, mix_ref[...], preferred_element_type=jnp.float32).astype(
        out_ref.dtype
    )


def shards(fields, coeffs, entries, band_info, conv_weight, mix_weight):
    band_index = lax.axis_index("lat")
    grid_rows = LAT_DEV * lax.axis_size("lat")
    nrows, nlon, members, channels = fields.shape
    coupling = band_coupling(entries, band_info, coeffs, band_index, grid_rows)
    coupling = coupling.astype(jnp.bfloat16).astype(jnp.float32)
    nwin = -(-nlon // WINDOW)
    pieces = []
    for piece, width, depth in zip(gather_pieces(fields), WIDTHS, DEPTHS):
        need = (nwin - 1) * WINDOW * width + depth
        pieces.append(jnp.pad(piece, ((0, need - piece.shape[0]), (0, 0))))
    out_rows = members * nlon * LAT_DEV
    toeplitz_rows = BASIS * LAT_DEV * LON_PAD
    mixed = pl.pallas_call(
        conv_mix_kernel,
        out_shape=jax.ShapeDtypeStruct((out_rows, CHANNELS), jnp.bfloat16),
        in_specs=[pl.BlockSpec(memory_space=pltpu.VMEM)] * 6,
        out_specs=pl.BlockSpec(memory_space=pltpu.VMEM),
        scratch_shapes=[pltpu.VMEM((BASIS * CHANNELS // 128, out_rows, 128), jnp.float32)]
        + [pltpu.VMEM((toeplitz_rows, depth), jnp.bfloat16) for depth in DEPTHS],
        cost_estimate=pl.CostEstimate(
            flops=2 * toeplitz_rows * sum(DEPTHS) * 1024 * nwin
            + 2 * out_rows * CHANNELS * CHANNELS * (BASIS + 1),
            transcendentals=out_rows * CHANNELS,
            bytes_accessed=sum(p.size for p in pieces) * 2 + (BASIS + 2) * CHANNELS * CHANNELS * 2,
        ),
    )(coupling, *pieces, conv_weight, mix_weight)
    return mixed.reshape(LAT_DEV, nlon, members, CHANNELS)


def solution(mesh):
    in_specs = (P("lat", "lon", None, None), P(), P(), P(), P(), P())
    out_specs = P("lat", "lon", None, None)
    return jax.shard_map(shards, mesh=mesh, in_specs=in_specs, out_specs=out_specs, check_vma=False)
```

```python
import jax
import jax.numpy as jnp
from jax import lax
from jax.experimental import pallas as pl
from jax.experimental.pallas import tpu as pltpu
from jax.sharding import PartitionSpec as P

CHANNELS = 512
BASIS = 3
SHIFTS = 7
OVERHANG = 3
LAT_DEV = 4
PIECE_LANES = 32


def band_coupling(entries, band_meta, coeffs, band_index, grid_rows):
    nbands = entries.shape[0]
    blocks = entries.shape[1]
    ids = band_index + jnp.arange(-1, 2, dtype=jnp.int32)
    known = (ids >= 0) & (ids < nbands)
    clamped = jnp.clip(ids, 0, nbands - 1)
    listed = jnp.take(entries, clamped, axis=0)
    meta = jnp.take(band_meta, clamped, axis=0)
    out_rows = listed[:, :, 0, :]
    in_rows = listed[:, :, 1, :]
    shifts = listed[:, :, 2, :]
    filter_rows = listed[:, :, 3, :]
    block_ids = jnp.arange(blocks, dtype=jnp.int32)[None, :, None]
    own_rel = out_rows - clamped[:, None, None] * LAT_DEV
    usable = known[:, None, None] & (block_ids < meta[:, 0, None, None])
    usable = usable & (own_rel >= -meta[:, 1, None, None])
    usable = usable & (own_rel < LAT_DEV + meta[:, 2, None, None])
    usable = usable & (out_rows >= 0) & (out_rows < grid_rows)
    band_start = band_index * LAT_DEV
    rows_in = LAT_DEV + 2 * OVERHANG
    q = out_rows - band_start
    r = in_rows - (band_start - OVERHANG)
    usable = usable & (q >= 0) & (q < LAT_DEV) & (r >= 0) & (r < rows_in)
    piece = (r >= OVERHANG).astype(jnp.int32) + (r >= OVERHANG + LAT_DEV).astype(jnp.int32)
    width = jnp.where(piece == 1, LAT_DEV, OVERHANG)
    local = r - jnp.where(piece == 0, 0, jnp.where(piece == 1, OVERHANG, OVERHANG + LAT_DEV))
    lane = q * 128 + piece * PIECE_LANES + (SHIFTS - 1 - shifts) * width + local
    slot = jnp.where(usable, lane, -1).reshape(-1)
    nslots = LAT_DEV * 128
    slot_hit = (slot[:, None] == jnp.arange(nslots, dtype=jnp.int32)[None, :]).astype(jnp.bfloat16)
    nfilters = coeffs.shape[0]
    filter_hit = (
        filter_rows.reshape(-1)[:, None] == jnp.arange(nfilters, dtype=jnp.int32)[None, :]
    ).astype(jnp.bfloat16)
    counts = lax.dot_general(
        filter_hit, slot_hit, (((0,), (0,)), ((), ())), preferred_element_type=jnp.float32
    )
    coupling = jnp.dot(
        coeffs.T, counts, precision=lax.Precision.HIGHEST, preferred_element_type=jnp.float32
    )
    return coupling


def lon_major(rows):
    count, nlon, members, channels = rows.shape
    return jnp.transpose(rows, (1, 0, 2, 3)).reshape(nlon * count, members * channels)


def gather_pieces(x):
    nlat = lax.axis_size("lat")
    nlon = lax.axis_size("lon")
    lo = SHIFTS - 1
    tail = x[:, x.shape[1] - lo :]

    def move(value, dlat, dlon):
        pairs = []
        for b in range(nlat):
            if 0 <= b + dlat < nlat:
                for j in range(nlon):
                    pairs.append((b * nlon + j, (b + dlat) * nlon + (j + dlon) % nlon))
        return lax.ppermute(value, ("lat", "lon"), pairs)

    below = move(x[LAT_DEV - OVERHANG :], 1, 0)
    above = move(x[:OVERHANG], -1, 0)
    below_left = move(tail[LAT_DEV - OVERHANG :], 1, 1)
    above_left = move(tail[:OVERHANG], -1, 1)
    left = move(tail, 0, 1)
    return (
        lon_major(jnp.concatenate([below_left, below], axis=1)),
        lon_major(jnp.concatenate([left, x], axis=1)),
        lon_major(jnp.concatenate([above_left, above], axis=1)),
    )


WINDOW = 32
LON_PAD = 32
TAPS = 128
WIDTHS = (OVERHANG, LAT_DEV, OVERHANG)
DEPTHS = (128, 256, 128)


def conv_mix_kernel(
    coupling_ref, below_ref, own_ref, above_ref, weight_ref, mix_ref, out_ref, feature_ref, *toeplitz_refs
):
    for p in range(3):
        width, depth = WIDTHS[p], DEPTHS[p]
        lane = lax.broadcasted_iota(jnp.int32, (1, TAPS), 1)
        for k in range(BASIS):
            for q in range(LAT_DEV):
                taps = coupling_ref[k : k + 1, q * TAPS : (q + 1) * TAPS]
                if p:
                    taps = pltpu.roll(taps, TAPS - p * PIECE_LANES, 1)
                taps = jnp.where(lane < SHIFTS * width, taps, 0.0)
                if depth > TAPS:
                    taps = jnp.concatenate([taps, jnp.zeros((1, depth - TAPS), jnp.float32)], axis=1)
                for g in range(LON_PAD // 8):
                    block = jnp.broadcast_to(taps, (8, depth))
                    if g:
                        block = pltpu.roll(block, 8 * g * width, 1)
                    block = pltpu.roll(block, 0, 1, stride=width, stride_axis=0)
                    toeplitz_refs[p][pl.ds((k * LAT_DEV + q) * LON_PAD + 8 * g, 8), :] = block.astype(
                        jnp.bfloat16
                    )
    nlon = out_ref.shape[0] // LAT_DEV
    nwin = -(-nlon // WINDOW)
    row_refs = (below_ref, own_ref, above_ref)
    for j in range(nwin):
        conv = None
        for p in range(3):
            window = row_refs[p][pl.ds(j * WINDOW * WIDTHS[p], DEPTHS[p]), :]
            term = jnp.dot(toeplitz_refs[p][...], window, preferred_element_type=jnp.float32)
            conv = term if conv is None else conv + term
        for k in range(BASIS):
            for q in range(LAT_DEV):
                count = min(WINDOW, nlon - j * WINDOW)
                first = (k * LAT_DEV + q) * LON_PAD
                block = conv[first : first + count]
                base = (q * nlon + j * WINDOW) * 2
                for m in range(2):
                    for c in range(CHANNELS // 128):
                        lanes = m * CHANNELS + c * 128
                        feature_ref[k * (CHANNELS // 128) + c, pl.ds(base + m, count, stride=2), :] = (
                            block[:, lanes : lanes + 128]
                        )
    combined = None
    for k in range(BASIS):
        features = jnp.concatenate(
            [feature_ref[k * (CHANNELS // 128) + c] for c in range(CHANNELS // 128)], axis=1
        ).astype(jnp.bfloat16)
        term = jnp.dot(
            features,
            weight_ref[k * CHANNELS : (k + 1) * CHANNELS, :],
            preferred_element_type=jnp.float32,
        )
        combined = term if combined is None else combined + term
    activated = jax.nn.gelu(combined, approximate=True).astype(jnp.bfloat16)
    mixed = jnp.dot(activated, mix_ref[...], preferred_element_type=jnp.float32).astype(out_ref.dtype)
    out_ref[...] = mixed.reshape(out_ref.shape)


def shards(fields, coeffs, entries, band_info, conv_weight, mix_weight):
    band_index = lax.axis_index("lat")
    grid_rows = LAT_DEV * lax.axis_size("lat")
    nrows, nlon, members, channels = fields.shape
    coupling = band_coupling(entries, band_info, coeffs, band_index, grid_rows)
    coupling = coupling.astype(jnp.bfloat16).astype(jnp.float32)
    nwin = -(-nlon // WINDOW)
    pieces = []
    for piece, width, depth in zip(gather_pieces(fields), WIDTHS, DEPTHS):
        need = (nwin - 1) * WINDOW * width + depth
        pieces.append(jnp.pad(piece, ((0, need - piece.shape[0]), (0, 0))))
    out_rows = members * nlon * LAT_DEV
    toeplitz_rows = BASIS * LAT_DEV * LON_PAD
    mixed = pl.pallas_call(
        conv_mix_kernel,
        out_shape=jax.ShapeDtypeStruct((LAT_DEV * nlon, members, CHANNELS), jnp.bfloat16),
        in_specs=[pl.BlockSpec(memory_space=pltpu.VMEM)] * 6,
        out_specs=pl.BlockSpec(memory_space=pltpu.VMEM),
        scratch_shapes=[pltpu.VMEM((BASIS * CHANNELS // 128, out_rows, 128), jnp.float32)]
        + [pltpu.VMEM((toeplitz_rows, depth), jnp.bfloat16) for depth in DEPTHS],
        cost_estimate=pl.CostEstimate(
            flops=2 * toeplitz_rows * sum(DEPTHS) * 1024 * nwin
            + 2 * out_rows * CHANNELS * CHANNELS * (BASIS + 1),
            transcendentals=out_rows * CHANNELS,
            bytes_accessed=sum(p.size for p in pieces) * 2 + (BASIS + 2) * CHANNELS * CHANNELS * 2,
        ),
    )(coupling, *pieces, conv_weight, mix_weight)
    return mixed.reshape(LAT_DEV, nlon, members, CHANNELS)


def solution(mesh):
    in_specs = (P("lat", "lon", None, None), P(), P(), P(), P(), P())
    out_specs = P("lat", "lon", None, None)
    return jax.shard_map(shards, mesh=mesh, in_specs=in_specs, out_specs=out_specs, check_vma=False)
```

```python
import jax
import jax.numpy as jnp
from jax import lax
from jax.experimental import pallas as pl
from jax.experimental.pallas import tpu as pltpu
from jax.sharding import PartitionSpec as P

CHANNELS = 512
BASIS = 3
SHIFTS = 7
OVERHANG = 3
LAT_DEV = 4
PIECE_LANES = 32


def band_coupling(entries, band_meta, coeffs, band_index, grid_rows):
    nbands = entries.shape[0]
    blocks = entries.shape[1]
    ids = band_index + jnp.arange(-1, 2, dtype=jnp.int32)
    known = (ids >= 0) & (ids < nbands)
    clamped = jnp.clip(ids, 0, nbands - 1)
    listed = jnp.take(entries, clamped, axis=0)
    meta = jnp.take(band_meta, clamped, axis=0)
    out_rows = listed[:, :, 0, :]
    in_rows = listed[:, :, 1, :]
    shifts = listed[:, :, 2, :]
    filter_rows = listed[:, :, 3, :]
    block_ids = jnp.arange(blocks, dtype=jnp.int32)[None, :, None]
    own_rel = out_rows - clamped[:, None, None] * LAT_DEV
    usable = known[:, None, None] & (block_ids < meta[:, 0, None, None])
    usable = usable & (own_rel >= -meta[:, 1, None, None])
    usable = usable & (own_rel < LAT_DEV + meta[:, 2, None, None])
    usable = usable & (out_rows >= 0) & (out_rows < grid_rows)
    band_start = band_index * LAT_DEV
    rows_in = LAT_DEV + 2 * OVERHANG
    q = out_rows - band_start
    r = in_rows - (band_start - OVERHANG)
    usable = usable & (q >= 0) & (q < LAT_DEV) & (r >= 0) & (r < rows_in)
    piece = (r >= OVERHANG).astype(jnp.int32) + (r >= OVERHANG + LAT_DEV).astype(jnp.int32)
    width = jnp.where(piece == 1, LAT_DEV, OVERHANG)
    local = r - jnp.where(piece == 0, 0, jnp.where(piece == 1, OVERHANG, OVERHANG + LAT_DEV))
    lane = q * 128 + piece * PIECE_LANES + (SHIFTS - 1 - shifts) * width + local
    slot = jnp.where(usable, lane, -1).reshape(-1)
    nslots = LAT_DEV * 128
    slot_hit = (slot[:, None] == jnp.arange(nslots, dtype=jnp.int32)[None, :]).astype(jnp.bfloat16)
    nfilters = coeffs.shape[0]
    filter_hit = (
        filter_rows.reshape(-1)[:, None] == jnp.arange(nfilters, dtype=jnp.int32)[None, :]
    ).astype(jnp.bfloat16)
    counts = lax.dot_general(
        filter_hit, slot_hit, (((0,), (0,)), ((), ())), preferred_element_type=jnp.float32
    )
    coupling = jnp.dot(
        coeffs.T, counts, precision=lax.Precision.HIGHEST, preferred_element_type=jnp.float32
    )
    return coupling


def lon_major(rows):
    count, nlon, members, channels = rows.shape
    return jnp.transpose(rows, (1, 0, 2, 3)).reshape(nlon * count, members * channels)


def gather_pieces(x):
    nlat = lax.axis_size("lat")
    nlon = lax.axis_size("lon")
    lo = SHIFTS - 1
    tail = x[:, x.shape[1] - lo :]

    def move(value, dlat, dlon):
        pairs = []
        for b in range(nlat):
            if 0 <= b + dlat < nlat:
                for j in range(nlon):
                    pairs.append((b * nlon + j, (b + dlat) * nlon + (j + dlon) % nlon))
        return lax.ppermute(value, ("lat", "lon"), pairs)

    below = move(x[LAT_DEV - OVERHANG :], 1, 0)
    above = move(x[:OVERHANG], -1, 0)
    left = move(tail, 0, 1)
    below_left = move(left[LAT_DEV - OVERHANG :], 1, 0)
    above_left = move(left[:OVERHANG], -1, 0)
    return (
        lon_major(jnp.concatenate([below_left, below], axis=1)),
        lon_major(jnp.concatenate([left, x], axis=1)),
        lon_major(jnp.concatenate([above_left, above], axis=1)),
    )


WINDOW = 32
LON_PAD = 32
TAPS = 128
WIDTHS = (OVERHANG, LAT_DEV, OVERHANG)
DEPTHS = (128, 256, 128)


def conv_mix_kernel(
    coupling_ref, below_ref, own_ref, above_ref, weight_ref, mix_ref, out_ref, feature_ref, *toeplitz_refs
):
    for p in range(3):
        width, depth = WIDTHS[p], DEPTHS[p]
        lane = lax.broadcasted_iota(jnp.int32, (1, TAPS), 1)
        for k in range(BASIS):
            for q in range(LAT_DEV):
                taps = coupling_ref[k : k + 1, q * TAPS : (q + 1) * TAPS]
                if p:
                    taps = pltpu.roll(taps, TAPS - p * PIECE_LANES, 1)
                taps = jnp.where(lane < SHIFTS * width, taps, 0.0)
                if depth > TAPS:
                    taps = jnp.concatenate([taps, jnp.zeros((1, depth - TAPS), jnp.float32)], axis=1)
                for g in range(LON_PAD // 8):
                    block = jnp.broadcast_to(taps, (8, depth))
                    if g:
                        block = pltpu.roll(block, 8 * g * width, 1)
                    block = pltpu.roll(block, 0, 1, stride=width, stride_axis=0)
                    toeplitz_refs[p][pl.ds((k * LAT_DEV + q) * LON_PAD + 8 * g, 8), :] = block.astype(
                        jnp.bfloat16
                    )
    nlon = out_ref.shape[0] // LAT_DEV
    nwin = -(-nlon // WINDOW)
    row_refs = (below_ref, own_ref, above_ref)
    for j in range(nwin):
        conv = None
        for p in range(3):
            window = row_refs[p][pl.ds(j * WINDOW * WIDTHS[p], DEPTHS[p]), :]
            term = jnp.dot(toeplitz_refs[p][...], window, preferred_element_type=jnp.float32)
            conv = term if conv is None else conv + term
        for k in range(BASIS):
            for q in range(LAT_DEV):
                count = min(WINDOW, nlon - j * WINDOW)
                first = (k * LAT_DEV + q) * LON_PAD
                block = conv[first : first + count]
                base = (q * nlon + j * WINDOW) * 2
                for m in range(2):
                    for c in range(CHANNELS // 128):
                        lanes = m * CHANNELS + c * 128
                        feature_ref[k * (CHANNELS // 128) + c, pl.ds(base + m, count, stride=2), :] = (
                            block[:, lanes : lanes + 128]
                        )
    combined = None
    for k in range(BASIS):
        features = jnp.concatenate(
            [feature_ref[k * (CHANNELS // 128) + c] for c in range(CHANNELS // 128)], axis=1
        ).astype(jnp.bfloat16)
        term = jnp.dot(
            features,
            weight_ref[k * CHANNELS : (k + 1) * CHANNELS, :],
            preferred_element_type=jnp.float32,
        )
        combined = term if combined is None else combined + term
    activated = jax.nn.gelu(combined, approximate=True).astype(jnp.bfloat16)
    mixed = jnp.dot(activated, mix_ref[...], preferred_element_type=jnp.float32).astype(out_ref.dtype)
    out_ref[...] = mixed.reshape(out_ref.shape)


def shards(fields, coeffs, entries, band_info, conv_weight, mix_weight):
    band_index = lax.axis_index("lat")
    grid_rows = LAT_DEV * lax.axis_size("lat")
    nrows, nlon, members, channels = fields.shape
    coupling = band_coupling(entries, band_info, coeffs, band_index, grid_rows)
    coupling = coupling.astype(jnp.bfloat16).astype(jnp.float32)
    nwin = -(-nlon // WINDOW)
    pieces = []
    for piece, width, depth in zip(gather_pieces(fields), WIDTHS, DEPTHS):
        need = (nwin - 1) * WINDOW * width + depth
        pieces.append(jnp.pad(piece, ((0, need - piece.shape[0]), (0, 0))))
    out_rows = members * nlon * LAT_DEV
    toeplitz_rows = BASIS * LAT_DEV * LON_PAD
    mixed = pl.pallas_call(
        conv_mix_kernel,
        out_shape=jax.ShapeDtypeStruct((LAT_DEV * nlon, members, CHANNELS), jnp.bfloat16),
        in_specs=[pl.BlockSpec(memory_space=pltpu.VMEM)] * 6,
        out_specs=pl.BlockSpec(memory_space=pltpu.VMEM),
        scratch_shapes=[pltpu.VMEM((BASIS * CHANNELS // 128, out_rows, 128), jnp.float32)]
        + [pltpu.VMEM((toeplitz_rows, depth), jnp.bfloat16) for depth in DEPTHS],
        cost_estimate=pl.CostEstimate(
            flops=2 * toeplitz_rows * sum(DEPTHS) * 1024 * nwin
            + 2 * out_rows * CHANNELS * CHANNELS * (BASIS + 1),
            transcendentals=out_rows * CHANNELS,
            bytes_accessed=sum(p.size for p in pieces) * 2 + (BASIS + 2) * CHANNELS * CHANNELS * 2,
        ),
    )(coupling, *pieces, conv_weight, mix_weight)
    return mixed.reshape(LAT_DEV, nlon, members, CHANNELS)


def solution(mesh):
    in_specs = (P("lat", "lon", None, None), P(), P(), P(), P(), P())
    out_specs = P("lat", "lon", None, None)
    return jax.shard_map(shards, mesh=mesh, in_specs=in_specs, out_specs=out_specs, check_vma=False)
```

```python
import jax
import jax.numpy as jnp
from jax import lax
from jax.experimental import pallas as pl
from jax.experimental.pallas import tpu as pltpu
from jax.sharding import PartitionSpec as P

CHANNELS = 512
BASIS = 3
SHIFTS = 7
OVERHANG = 3
LAT_DEV = 4
PIECE_LANES = 32


def band_coupling(entries, band_meta, coeffs, band_index, grid_rows):
    nbands = entries.shape[0]
    blocks = entries.shape[1]
    ids = band_index + jnp.arange(-1, 2, dtype=jnp.int32)
    known = (ids >= 0) & (ids < nbands)
    clamped = jnp.clip(ids, 0, nbands - 1)
    listed = jnp.take(entries, clamped, axis=0)
    meta = jnp.take(band_meta, clamped, axis=0)
    out_rows = listed[:, :, 0, :]
    in_rows = listed[:, :, 1, :]
    shifts = listed[:, :, 2, :]
    filter_rows = listed[:, :, 3, :]
    block_ids = jnp.arange(blocks, dtype=jnp.int32)[None, :, None]
    own_rel = out_rows - clamped[:, None, None] * LAT_DEV
    usable = known[:, None, None] & (block_ids < meta[:, 0, None, None])
    usable = usable & (own_rel >= -meta[:, 1, None, None])
    usable = usable & (own_rel < LAT_DEV + meta[:, 2, None, None])
    usable = usable & (out_rows >= 0) & (out_rows < grid_rows)
    band_start = band_index * LAT_DEV
    rows_in = LAT_DEV + 2 * OVERHANG
    q = out_rows - band_start
    r = in_rows - (band_start - OVERHANG)
    usable = usable & (q >= 0) & (q < LAT_DEV) & (r >= 0) & (r < rows_in)
    piece = (r >= OVERHANG).astype(jnp.int32) + (r >= OVERHANG + LAT_DEV).astype(jnp.int32)
    width = jnp.where(piece == 1, LAT_DEV, OVERHANG)
    local = r - jnp.where(piece == 0, 0, jnp.where(piece == 1, OVERHANG, OVERHANG + LAT_DEV))
    lane = q * 128 + piece * PIECE_LANES + (SHIFTS - 1 - shifts) * width + local
    slot = jnp.where(usable, lane, -1).reshape(-1)
    nslots = LAT_DEV * 128
    slot_hit = (slot[:, None] == jnp.arange(nslots, dtype=jnp.int32)[None, :]).astype(jnp.bfloat16)
    nfilters = coeffs.shape[0]
    filter_hit = (
        filter_rows.reshape(-1)[:, None] == jnp.arange(nfilters, dtype=jnp.int32)[None, :]
    ).astype(jnp.bfloat16)
    counts = lax.dot_general(
        filter_hit, slot_hit, (((0,), (0,)), ((), ())), preferred_element_type=jnp.float32
    )
    coupling = jnp.dot(
        coeffs.T, counts, precision=lax.Precision.HIGHEST, preferred_element_type=jnp.float32
    )
    return coupling


def lon_major(rows):
    count, nlon, members, channels = rows.shape
    return jnp.transpose(rows, (1, 0, 2, 3)).reshape(nlon * count, members * channels)


def gather_pieces(x):
    nlat = lax.axis_size("lat")
    nlon = lax.axis_size("lon")
    lo = SHIFTS - 1
    tail = x[:, x.shape[1] - lo :]

    def move(value, dlat, dlon):
        pairs = []
        for b in range(nlat):
            if 0 <= b + dlat < nlat:
                for j in range(nlon):
                    pairs.append((b * nlon + j, (b + dlat) * nlon + (j + dlon) % nlon))
        return lax.ppermute(value, ("lat", "lon"), pairs)

    below = move(x[LAT_DEV - OVERHANG :], 1, 0)
    above = move(x[:OVERHANG], -1, 0)
    below_left = move(tail[LAT_DEV - OVERHANG :], 1, 1)
    above_left = move(tail[:OVERHANG], -1, 1)
    left = move(tail, 0, 1)
    return (
        lon_major(jnp.concatenate([below_left, below], axis=1)),
        lon_major(jnp.concatenate([left, x], axis=1)),
        lon_major(jnp.concatenate([above_left, above], axis=1)),
    )


WINDOW = 32
LON_PAD = 32
TAPS = 128
WIDTHS = (OVERHANG, LAT_DEV, OVERHANG)
DEPTHS = (128, 160, 128)
LANES = (128, 256, 128)


def conv_mix_kernel(
    coupling_ref, below_ref, own_ref, above_ref, weight_ref, mix_ref, out_ref, feature_ref, *toeplitz_refs
):
    for p in range(3):
        width, depth = WIDTHS[p], LANES[p]
        lane = lax.broadcasted_iota(jnp.int32, (1, TAPS), 1)
        for k in range(BASIS):
            for q in range(LAT_DEV):
                taps = coupling_ref[k : k + 1, q * TAPS : (q + 1) * TAPS]
                if p:
                    taps = pltpu.roll(taps, TAPS - p * PIECE_LANES, 1)
                taps = jnp.where(lane < SHIFTS * width, taps, 0.0)
                if depth > TAPS:
                    taps = jnp.concatenate([taps, jnp.zeros((1, depth - TAPS), jnp.float32)], axis=1)
                for g in range(LON_PAD // 8):
                    block = jnp.broadcast_to(taps, (8, depth))
                    if g:
                        block = pltpu.roll(block, 8 * g * width, 1)
                    block = pltpu.roll(block, 0, 1, stride=width, stride_axis=0)
                    toeplitz_refs[p][pl.ds((k * LAT_DEV + q) * LON_PAD + 8 * g, 8), :] = block.astype(
                        jnp.bfloat16
                    )
    nlon = out_ref.shape[0] // LAT_DEV
    nwin = -(-nlon // WINDOW)
    row_refs = (below_ref, own_ref, above_ref)
    for j in range(nwin):
        conv = None
        for p in range(3):
            window = row_refs[p][pl.ds(j * WINDOW * WIDTHS[p], DEPTHS[p]), :]
            term = jnp.dot(
                toeplitz_refs[p][:, : DEPTHS[p]], window, preferred_element_type=jnp.float32
            )
            conv = term if conv is None else conv + term
        for k in range(BASIS):
            for q in range(LAT_DEV):
                count = min(WINDOW, nlon - j * WINDOW)
                first = (k * LAT_DEV + q) * LON_PAD
                block = conv[first : first + count]
                base = (q * nlon + j * WINDOW) * 2
                for m in range(2):
                    for c in range(CHANNELS // 128):
                        lanes = m * CHANNELS + c * 128
                        feature_ref[k * (CHANNELS // 128) + c, pl.ds(base + m, count, stride=2), :] = (
                            block[:, lanes : lanes + 128]
                        )
    combined = None
    for k in range(BASIS):
        features = jnp.concatenate(
            [feature_ref[k * (CHANNELS // 128) + c] for c in range(CHANNELS // 128)], axis=1
        ).astype(jnp.bfloat16)
        term = jnp.dot(
            features,
            weight_ref[k * CHANNELS : (k + 1) * CHANNELS, :],
            preferred_element_type=jnp.float32,
        )
        combined = term if combined is None else combined + term
    activated = jax.nn.gelu(combined, approximate=True).astype(jnp.bfloat16)
    mixed = jnp.dot(activated, mix_ref[...], preferred_element_type=jnp.float32).astype(out_ref.dtype)
    out_ref[...] = mixed.reshape(out_ref.shape)


def shards(fields, coeffs, entries, band_info, conv_weight, mix_weight):
    band_index = lax.axis_index("lat")
    grid_rows = LAT_DEV * lax.axis_size("lat")
    nrows, nlon, members, channels = fields.shape
    coupling = band_coupling(entries, band_info, coeffs, band_index, grid_rows)
    coupling = coupling.astype(jnp.bfloat16).astype(jnp.float32)
    nwin = -(-nlon // WINDOW)
    pieces = []
    for piece, width, depth in zip(gather_pieces(fields), WIDTHS, DEPTHS):
        need = (nwin - 1) * WINDOW * width + depth
        pieces.append(jnp.pad(piece, ((0, need - piece.shape[0]), (0, 0))))
    out_rows = members * nlon * LAT_DEV
    toeplitz_rows = BASIS * LAT_DEV * LON_PAD
    mixed = pl.pallas_call(
        conv_mix_kernel,
        out_shape=jax.ShapeDtypeStruct((LAT_DEV * nlon, members, CHANNELS), jnp.bfloat16),
        in_specs=[pl.BlockSpec(memory_space=pltpu.VMEM)] * 6,
        out_specs=pl.BlockSpec(memory_space=pltpu.VMEM),
        scratch_shapes=[pltpu.VMEM((BASIS * CHANNELS // 128, out_rows, 128), jnp.float32)]
        + [pltpu.VMEM((toeplitz_rows, lanes), jnp.bfloat16) for lanes in LANES],
        cost_estimate=pl.CostEstimate(
            flops=2 * toeplitz_rows * sum(DEPTHS) * 1024 * nwin
            + 2 * out_rows * CHANNELS * CHANNELS * (BASIS + 1),
            transcendentals=out_rows * CHANNELS,
            bytes_accessed=sum(p.size for p in pieces) * 2 + (BASIS + 2) * CHANNELS * CHANNELS * 2,
        ),
    )(coupling, *pieces, conv_weight, mix_weight)
    return mixed.reshape(LAT_DEV, nlon, members, CHANNELS)


def solution(mesh):
    in_specs = (P("lat", "lon", None, None), P(), P(), P(), P(), P())
    out_specs = P("lat", "lon", None, None)
    return jax.shard_map(shards, mesh=mesh, in_specs=in_specs, out_specs=out_specs, check_vma=False)
```

```python
import jax
import jax.numpy as jnp
from jax import lax
from jax.experimental import pallas as pl
from jax.experimental.pallas import tpu as pltpu
from jax.sharding import PartitionSpec as P

CHANNELS = 512
BASIS = 3
SHIFTS = 7
OVERHANG = 3
LAT_DEV = 4
PIECE_LANES = 32


def band_coupling(entries, band_meta, coeffs, band_index, grid_rows):
    nbands = entries.shape[0]
    blocks = entries.shape[1]
    ids = band_index + jnp.arange(-1, 2, dtype=jnp.int32)
    known = (ids >= 0) & (ids < nbands)
    clamped = jnp.clip(ids, 0, nbands - 1)
    listed = jnp.take(entries, clamped, axis=0)
    meta = jnp.take(band_meta, clamped, axis=0)
    out_rows = listed[:, :, 0, :]
    in_rows = listed[:, :, 1, :]
    shifts = listed[:, :, 2, :]
    filter_rows = listed[:, :, 3, :]
    block_ids = jnp.arange(blocks, dtype=jnp.int32)[None, :, None]
    own_rel = out_rows - clamped[:, None, None] * LAT_DEV
    usable = known[:, None, None] & (block_ids < meta[:, 0, None, None])
    usable = usable & (own_rel >= -meta[:, 1, None, None])
    usable = usable & (own_rel < LAT_DEV + meta[:, 2, None, None])
    usable = usable & (out_rows >= 0) & (out_rows < grid_rows)
    band_start = band_index * LAT_DEV
    rows_in = LAT_DEV + 2 * OVERHANG
    q = out_rows - band_start
    r = in_rows - (band_start - OVERHANG)
    usable = usable & (q >= 0) & (q < LAT_DEV) & (r >= 0) & (r < rows_in)
    piece = (r >= OVERHANG).astype(jnp.int32) + (r >= OVERHANG + LAT_DEV).astype(jnp.int32)
    width = jnp.where(piece == 1, LAT_DEV, OVERHANG)
    local = r - jnp.where(piece == 0, 0, jnp.where(piece == 1, OVERHANG, OVERHANG + LAT_DEV))
    lane = q * 128 + piece * PIECE_LANES + (SHIFTS - 1 - shifts) * width + local
    slot = jnp.where(usable, lane, -1).reshape(-1)
    nslots = LAT_DEV * 128
    slot_hit = (slot[:, None] == jnp.arange(nslots, dtype=jnp.int32)[None, :]).astype(jnp.bfloat16)
    nfilters = coeffs.shape[0]
    filter_hit = (
        filter_rows.reshape(-1)[:, None] == jnp.arange(nfilters, dtype=jnp.int32)[None, :]
    ).astype(jnp.bfloat16)
    counts = lax.dot_general(
        filter_hit, slot_hit, (((0,), (0,)), ((), ())), preferred_element_type=jnp.float32
    )
    coupling = jnp.dot(
        coeffs.T, counts, precision=lax.Precision.HIGHEST, preferred_element_type=jnp.float32
    )
    return coupling


def lon_major(rows):
    count, nlon, members, channels = rows.shape
    return jnp.transpose(rows, (1, 0, 2, 3)).reshape(nlon * count, members * channels)


def gather_pieces(x):
    nlat = lax.axis_size("lat")
    nlon = lax.axis_size("lon")
    lo = SHIFTS - 1
    tail = x[:, x.shape[1] - lo :]

    def move(value, dlat, dlon):
        pairs = []
        for b in range(nlat):
            if 0 <= b + dlat < nlat:
                for j in range(nlon):
                    pairs.append((b * nlon + j, (b + dlat) * nlon + (j + dlon) % nlon))
        return lax.ppermute(value, ("lat", "lon"), pairs)

    below = move(x[LAT_DEV - OVERHANG :], 1, 0)
    above = move(x[:OVERHANG], -1, 0)
    below_left = move(tail[LAT_DEV - OVERHANG :], 1, 1)
    above_left = move(tail[:OVERHANG], -1, 1)
    left = move(tail, 0, 1)
    return (
        lon_major(jnp.concatenate([below_left, below], axis=1)),
        lon_major(jnp.concatenate([left, x], axis=1)),
        lon_major(jnp.concatenate([above_left, above], axis=1)),
    )


WINDOW = 32
LON_PAD = 32
TAPS = 128
WIDTHS = (OVERHANG, LAT_DEV, OVERHANG)
DEPTHS = (128, 160, 128)
LANES = (128, 256, 128)


def toeplitz_kernel(coupling_ref, *toeplitz_refs):
    for p in range(3):
        width, depth = WIDTHS[p], LANES[p]
        lane = lax.broadcasted_iota(jnp.int32, (1, TAPS), 1)
        for k in range(BASIS):
            for q in range(LAT_DEV):
                taps = coupling_ref[k : k + 1, q * TAPS : (q + 1) * TAPS]
                if p:
                    taps = pltpu.roll(taps, TAPS - p * PIECE_LANES, 1)
                taps = jnp.where(lane < SHIFTS * width, taps, 0.0)
                if depth > TAPS:
                    taps = jnp.concatenate([taps, jnp.zeros((1, depth - TAPS), jnp.float32)], axis=1)
                for g in range(LON_PAD // 8):
                    block = jnp.broadcast_to(taps, (8, depth))
                    if g:
                        block = pltpu.roll(block, 8 * g * width, 1)
                    block = pltpu.roll(block, 0, 1, stride=width, stride_axis=0)
                    toeplitz_refs[p][pl.ds((k * LAT_DEV + q) * LON_PAD + 8 * g, 8), :] = block.astype(
                        jnp.bfloat16
                    )


def conv_mix_kernel(
    below_t_ref, own_t_ref, above_t_ref, below_ref, own_ref, above_ref, weight_ref, mix_ref, out_ref, feature_ref
):
    toeplitz_refs = (below_t_ref, own_t_ref, above_t_ref)
    nlon = out_ref.shape[0] // LAT_DEV
    nwin = -(-nlon // WINDOW)
    row_refs = (below_ref, own_ref, above_ref)
    for j in range(nwin):
        conv = None
        for p in range(3):
            window = row_refs[p][pl.ds(j * WINDOW * WIDTHS[p], DEPTHS[p]), :]
            term = jnp.dot(
                toeplitz_refs[p][:, : DEPTHS[p]], window, preferred_element_type=jnp.float32
            )
            conv = term if conv is None else conv + term
        for k in range(BASIS):
            for q in range(LAT_DEV):
                count = min(WINDOW, nlon - j * WINDOW)
                first = (k * LAT_DEV + q) * LON_PAD
                block = conv[first : first + count]
                base = (q * nlon + j * WINDOW) * 2
                for m in range(2):
                    for c in range(CHANNELS // 128):
                        lanes = m * CHANNELS + c * 128
                        feature_ref[k * (CHANNELS // 128) + c, pl.ds(base + m, count, stride=2), :] = (
                            block[:, lanes : lanes + 128]
                        )
    combined = None
    for k in range(BASIS):
        features = jnp.concatenate(
            [feature_ref[k * (CHANNELS // 128) + c] for c in range(CHANNELS // 128)], axis=1
        ).astype(jnp.bfloat16)
        term = jnp.dot(
            features,
            weight_ref[k * CHANNELS : (k + 1) * CHANNELS, :],
            preferred_element_type=jnp.float32,
        )
        combined = term if combined is None else combined + term
    activated = jax.nn.gelu(combined, approximate=True).astype(jnp.bfloat16)
    mixed = jnp.dot(activated, mix_ref[...], preferred_element_type=jnp.float32).astype(out_ref.dtype)
    out_ref[...] = mixed.reshape(out_ref.shape)


def shards(fields, coeffs, entries, band_info, conv_weight, mix_weight):
    band_index = lax.axis_index("lat")
    grid_rows = LAT_DEV * lax.axis_size("lat")
    nrows, nlon, members, channels = fields.shape
    coupling = band_coupling(entries, band_info, coeffs, band_index, grid_rows)
    coupling = coupling.astype(jnp.bfloat16).astype(jnp.float32)
    nwin = -(-nlon // WINDOW)
    pieces = []
    for piece, width, depth in zip(gather_pieces(fields), WIDTHS, DEPTHS):
        need = (nwin - 1) * WINDOW * width + depth
        pieces.append(jnp.pad(piece, ((0, need - piece.shape[0]), (0, 0))))
    out_rows = members * nlon * LAT_DEV
    toeplitz_rows = BASIS * LAT_DEV * LON_PAD
    toeplitz = pl.pallas_call(
        toeplitz_kernel,
        out_shape=[jax.ShapeDtypeStruct((toeplitz_rows, lanes), jnp.bfloat16) for lanes in LANES],
        in_specs=[pl.BlockSpec(memory_space=pltpu.VMEM)],
        out_specs=[pl.BlockSpec(memory_space=pltpu.VMEM)] * 3,
        cost_estimate=pl.CostEstimate(
            flops=0, transcendentals=0, bytes_accessed=toeplitz_rows * sum(LANES) * 2
        ),
    )(coupling)
    mixed = pl.pallas_call(
        conv_mix_kernel,
        out_shape=jax.ShapeDtypeStruct((LAT_DEV * nlon, members, CHANNELS), jnp.bfloat16),
        in_specs=[pl.BlockSpec(memory_space=pltpu.VMEM)] * 8,
        out_specs=pl.BlockSpec(memory_space=pltpu.VMEM),
        scratch_shapes=[pltpu.VMEM((BASIS * CHANNELS // 128, out_rows, 128), jnp.float32)],
        cost_estimate=pl.CostEstimate(
            flops=2 * toeplitz_rows * sum(DEPTHS) * 1024 * nwin
            + 2 * out_rows * CHANNELS * CHANNELS * (BASIS + 1),
            transcendentals=out_rows * CHANNELS,
            bytes_accessed=sum(p.size for p in pieces) * 2 + (BASIS + 2) * CHANNELS * CHANNELS * 2,
        ),
    )(*toeplitz, *pieces, conv_weight, mix_weight)
    return mixed.reshape(LAT_DEV, nlon, members, CHANNELS)


def solution(mesh):
    in_specs = (P("lat", "lon", None, None), P(), P(), P(), P(), P())
    out_specs = P("lat", "lon", None, None)
    return jax.shard_map(shards, mesh=mesh, in_specs=in_specs, out_specs=out_specs, check_vma=False)
```

```python
import jax
import jax.numpy as jnp
from jax import lax
from jax.experimental import pallas as pl
from jax.experimental.pallas import tpu as pltpu
from jax.sharding import PartitionSpec as P

CHANNELS = 512
BASIS = 3
SHIFTS = 7
OVERHANG = 3
LAT_DEV = 4
PIECE_LANES = 32


def band_coupling(entries, band_meta, coeffs, band_index, grid_rows):
    nbands = entries.shape[0]
    blocks = entries.shape[1]
    ids = band_index + jnp.arange(-1, 2, dtype=jnp.int32)
    known = (ids >= 0) & (ids < nbands)
    clamped = jnp.clip(ids, 0, nbands - 1)
    listed = jnp.take(entries, clamped, axis=0)
    meta = jnp.take(band_meta, clamped, axis=0)
    out_rows = listed[:, :, 0, :]
    in_rows = listed[:, :, 1, :]
    shifts = listed[:, :, 2, :]
    filter_rows = listed[:, :, 3, :]
    block_ids = jnp.arange(blocks, dtype=jnp.int32)[None, :, None]
    own_rel = out_rows - clamped[:, None, None] * LAT_DEV
    usable = known[:, None, None] & (block_ids < meta[:, 0, None, None])
    usable = usable & (own_rel >= -meta[:, 1, None, None])
    usable = usable & (own_rel < LAT_DEV + meta[:, 2, None, None])
    usable = usable & (out_rows >= 0) & (out_rows < grid_rows)
    band_start = band_index * LAT_DEV
    rows_in = LAT_DEV + 2 * OVERHANG
    q = out_rows - band_start
    r = in_rows - (band_start - OVERHANG)
    usable = usable & (q >= 0) & (q < LAT_DEV) & (r >= 0) & (r < rows_in)
    piece = (r >= OVERHANG).astype(jnp.int32) + (r >= OVERHANG + LAT_DEV).astype(jnp.int32)
    width = jnp.where(piece == 1, LAT_DEV, OVERHANG)
    local = r - jnp.where(piece == 0, 0, jnp.where(piece == 1, OVERHANG, OVERHANG + LAT_DEV))
    lane = q * 128 + piece * PIECE_LANES + (SHIFTS - 1 - shifts) * width + local
    slot = jnp.where(usable, lane, -1).reshape(-1)
    nslots = LAT_DEV * 128
    slot_hit = (slot[:, None] == jnp.arange(nslots, dtype=jnp.int32)[None, :]).astype(jnp.bfloat16)
    nfilters = coeffs.shape[0]
    filter_hit = (
        filter_rows.reshape(-1)[:, None] == jnp.arange(nfilters, dtype=jnp.int32)[None, :]
    ).astype(jnp.bfloat16)
    counts = lax.dot_general(
        filter_hit, slot_hit, (((0,), (0,)), ((), ())), preferred_element_type=jnp.float32
    )
    coupling = jnp.dot(
        coeffs.T, counts, precision=lax.Precision.HIGHEST, preferred_element_type=jnp.float32
    )
    return coupling


def lon_major(rows):
    count, nlon, members, channels = rows.shape
    return jnp.transpose(rows, (1, 0, 2, 3)).reshape(nlon * count, members * channels)


def gather_pieces(x):
    nlat = lax.axis_size("lat")
    nlon = lax.axis_size("lon")
    lo = SHIFTS - 1
    left = lax.ppermute(x[:, x.shape[1] - lo :], "lon", [(j, (j + 1) % nlon) for j in range(nlon)])
    ext = jnp.concatenate([left, x], axis=1)
    down = [(b, b + 1) for b in range(nlat - 1)]
    below = lax.ppermute(ext[LAT_DEV - OVERHANG :], "lat", down)
    above = lax.ppermute(ext[:OVERHANG], "lat", [(t, s) for s, t in down])
    return lon_major(below), lon_major(ext), lon_major(above)


WINDOW = 32
LON_PAD = 32
TAPS = 128
WIDTHS = (OVERHANG, LAT_DEV, OVERHANG)
DEPTHS = (128, 160, 128)
LANES = (128, 256, 128)


def conv_mix_kernel(
    coupling_ref, below_ref, own_ref, above_ref, weight_ref, mix_ref, out_ref, feature_ref, *toeplitz_refs
):
    for p in range(3):
        width, depth = WIDTHS[p], LANES[p]
        lane = lax.broadcasted_iota(jnp.int32, (1, TAPS), 1)
        for k in range(BASIS):
            for q in range(LAT_DEV):
                taps = coupling_ref[k : k + 1, q * TAPS : (q + 1) * TAPS]
                if p:
                    taps = pltpu.roll(taps, TAPS - p * PIECE_LANES, 1)
                taps = jnp.where(lane < SHIFTS * width, taps, 0.0)
                if depth > TAPS:
                    taps = jnp.concatenate([taps, jnp.zeros((1, depth - TAPS), jnp.float32)], axis=1)
                for g in range(LON_PAD // 8):
                    block = jnp.broadcast_to(taps, (8, depth))
                    if g:
                        block = pltpu.roll(block, 8 * g * width, 1)
                    block = pltpu.roll(block, 0, 1, stride=width, stride_axis=0)
                    toeplitz_refs[p][pl.ds((k * LAT_DEV + q) * LON_PAD + 8 * g, 8), :] = block.astype(
                        jnp.bfloat16
                    )
    nlon = out_ref.shape[0] // LAT_DEV
    nwin = -(-nlon // WINDOW)
    row_refs = (below_ref, own_ref, above_ref)
    for j in range(nwin):
        conv = None
        for p in range(3):
            window = row_refs[p][pl.ds(j * WINDOW * WIDTHS[p], DEPTHS[p]), :]
            term = jnp.dot(
                toeplitz_refs[p][:, : DEPTHS[p]], window, preferred_element_type=jnp.float32
            )
            conv = term if conv is None else conv + term
        for k in range(BASIS):
            for q in range(LAT_DEV):
                count = min(WINDOW, nlon - j * WINDOW)
                first = (k * LAT_DEV + q) * LON_PAD
                block = conv[first : first + count]
                base = (q * nlon + j * WINDOW) * 2
                for m in range(2):
                    for c in range(CHANNELS // 128):
                        lanes = m * CHANNELS + c * 128
                        feature_ref[k * (CHANNELS // 128) + c, pl.ds(base + m, count, stride=2), :] = (
                            block[:, lanes : lanes + 128]
                        )
    combined = None
    for k in range(BASIS):
        features = jnp.concatenate(
            [feature_ref[k * (CHANNELS // 128) + c] for c in range(CHANNELS // 128)], axis=1
        ).astype(jnp.bfloat16)
        term = jnp.dot(
            features,
            weight_ref[k * CHANNELS : (k + 1) * CHANNELS, :],
            preferred_element_type=jnp.float32,
        )
        combined = term if combined is None else combined + term
    activated = jax.nn.gelu(combined, approximate=True).astype(jnp.bfloat16)
    mixed = jnp.dot(activated, mix_ref[...], preferred_element_type=jnp.float32).astype(out_ref.dtype)
    out_ref[...] = mixed.reshape(out_ref.shape)


def shards(fields, coeffs, entries, band_info, conv_weight, mix_weight):
    band_index = lax.axis_index("lat")
    grid_rows = LAT_DEV * lax.axis_size("lat")
    nrows, nlon, members, channels = fields.shape
    coupling = band_coupling(entries, band_info, coeffs, band_index, grid_rows)
    coupling = coupling.astype(jnp.bfloat16).astype(jnp.float32)
    nwin = -(-nlon // WINDOW)
    pieces = []
    for piece, width, depth in zip(gather_pieces(fields), WIDTHS, DEPTHS):
        need = (nwin - 1) * WINDOW * width + depth
        pieces.append(jnp.pad(piece, ((0, need - piece.shape[0]), (0, 0))))
    out_rows = members * nlon * LAT_DEV
    toeplitz_rows = BASIS * LAT_DEV * LON_PAD
    mixed = pl.pallas_call(
        conv_mix_kernel,
        out_shape=jax.ShapeDtypeStruct((LAT_DEV * nlon, members, CHANNELS), jnp.bfloat16),
        in_specs=[pl.BlockSpec(memory_space=pltpu.VMEM)] * 6,
        out_specs=pl.BlockSpec(memory_space=pltpu.VMEM),
        scratch_shapes=[pltpu.VMEM((BASIS * CHANNELS // 128, out_rows, 128), jnp.float32)]
        + [pltpu.VMEM((toeplitz_rows, lanes), jnp.bfloat16) for lanes in LANES],
        cost_estimate=pl.CostEstimate(
            flops=2 * toeplitz_rows * sum(DEPTHS) * 1024 * nwin
            + 2 * out_rows * CHANNELS * CHANNELS * (BASIS + 1),
            transcendentals=out_rows * CHANNELS,
            bytes_accessed=sum(p.size for p in pieces) * 2 + (BASIS + 2) * CHANNELS * CHANNELS * 2,
        ),
    )(coupling, *pieces, conv_weight, mix_weight)
    return mixed.reshape(LAT_DEV, nlon, members, CHANNELS)


def solution(mesh):
    in_specs = (P("lat", "lon", None, None), P(), P(), P(), P(), P())
    out_specs = P("lat", "lon", None, None)
    return jax.shard_map(shards, mesh=mesh, in_specs=in_specs, out_specs=out_specs, check_vma=False)
```
